128 devices in a mesh: gx: 16 (over x, z), gy: 8 (over y, core).
Axes of the slice: x: 4, y: 4, z: 4, core: 2. Of those that a mesh axis runs over, the one named last changes fastest.
Arguments:
- innovations: float32 [2, 128, 65536], P(None, None, ('gx', 'gy')), may hold values from -18 to 18
- obs_column: int32 [65536], P(('gx', 'gy')), may hold values from 0 to 4095
- obs_scale: float32 [2, 128], replicated, may hold values from 0.25 to 4
- band_of_lat: int32 [512], P('gy'), may hold values from 0 to 7, as said below
- balance: bfloat16 [8, 2, 128, 128], replicated, may hold values from -0.3 to 1.5
- lon_filter: bfloat16 [2, 1024, 1024], replicated, may hold values from 0 to 1
- lat_filter: bfloat16 [2, 512, 512], replicated, may hold values from 0 to 1
Outputs:
- control: float32 [2, 128, 1024, 512], P(None, ('gx', 'gy'))
- increment: float32 [2, 128, 1024, 512], P(None, None, 'gx', 'gy')
The draws below stay inside these ranges and needn't reach their ends.
Inputs may be any that keep to these rules, and one draw needn't show every extreme that they name: `obs_column`: column c of a tile lies at longitude offset c // 64 and latitude offset c % 64 within the tile. `band_of_lat`: never falls from one latitude to the next.
All inputs are finite; a program needn't handle non-finite values.
Results may differ from the reference program's by a relative error of at most 0.0049.
Values may be sent and summed in bfloat16 or wider, within the bound.
No kernel may reach another device: no remote copies, remote signals or barrier semaphores. Data moves between devices by JAX's collectives and lax.ppermute only.
A program may use at most 128 MiB of HBM per device.

```python
import math
import jax
import jax.numpy as jnp
from jax import lax

NLON = 1024
NLAT = 512
NLEV = 128
NVAR = 2
NBAND = 8
OBS_DEV = 512
ITERS = 2
LON_T = 64
LAT_T = 64
COLS_T = 4096
NOBS = 65536
N_GY = 8


def draw_innovations(key, part):
    key_main = jax.random.fold_in(key, 0)
    tile_index = jnp.arange(NOBS, dtype=jnp.int32) // OBS_DEV
    growth = 1.0 + 2.0 * tile_index.astype(jnp.float32) / max(NOBS // OBS_DEV - 1, 1)
    values = jax.random.normal(key_main, (NVAR, NLEV, NOBS), jnp.float32)
    return (jnp.clip(values, -6.0, 6.0) * growth[None, None, :]).astype(jnp.float32)


def draw_obs_scale(key, part):
    level_pos = jnp.arange(NLEV, dtype=jnp.float32) / max(NLEV - 1, 1)
    noise = jax.random.uniform(key, (NVAR, NLEV), jnp.float32, -0.3, 0.3)
    return (0.6 * jnp.exp(noise) * jnp.power(3.0, level_pos)[None, :]).astype(jnp.float32)


def draw_band_of_lat(key, part):
    jitter = NLAT // (4 * NBAND)
    bounds = jnp.arange(1, NBAND, dtype=jnp.int32) * NLAT // NBAND
    bounds = bounds + jax.random.randint(key, (NBAND - 1,), -jitter, jitter + 1, dtype=jnp.int32)
    rows = jnp.arange(NLAT, dtype=jnp.int32)
    return jnp.sum((rows[:, None] >= bounds[None, :]).astype(jnp.int32), axis=1).astype(jnp.int32)


def draw_balance(key, part):
    key_diag, key_off = jax.random.split(key)
    diagonal = jax.random.uniform(key_diag, (NBAND, NVAR, NLEV, 1), jnp.float32, 0.8, 1.2)
    rows = jnp.arange(NLEV, dtype=jnp.int32)
    identity = (rows[:, None] == rows[None, :]).astype(jnp.float32)
    offdiag = jnp.clip(jax.random.normal(key_off, (NBAND, NVAR, NLEV, NLEV), jnp.float32), -5.0, 5.0)
    offdiag = offdiag * (0.6 / math.sqrt(NLEV))
    return (identity * diagonal + offdiag).astype(jnp.bfloat16)


def line_filter(key, length, periodic):
    rows = jnp.arange(length, dtype=jnp.float32)
    distance = jnp.abs(rows[:, None] - rows[None, :])
    if periodic:
        distance = jnp.minimum(distance, length - distance)
    kernel = jnp.zeros((length, length), jnp.float32)
    for weight_part, width_part in ((0.5, 2.0), (0.3, max(length / 32.0, 1.0)), (0.2, max(length / 6.0, 1.0))):
        kernel = kernel + weight_part * jnp.exp(-distance * distance / (2.0 * width_part * width_part)) / (math.sqrt(2.0 * math.pi) * width_part)
    identity = (rows[:, None] == rows[None, :]).astype(jnp.float32)
    factor = jax.random.uniform(key, (NVAR, length, length), jnp.float32, 0.5, 1.5)
    return ((0.3 * identity + 0.7 * kernel)[None, :, :] * factor).astype(jnp.bfloat16)


def draw_lon_filter(key, part):
    return line_filter(key, NLON, True)


def draw_lat_filter(key, part):
    return line_filter(key, NLAT, False)


def place_ends(values, stream_key, low, high):
    place = [jax.random.randint(jax.random.fold_in(stream_key, axis), (), 0, length) for axis, length in enumerate(values.shape)]
    widest = values.shape.index(max(values.shape))
    next_to = place[:widest] + [(place[widest] + 1) % values.shape[widest]] + place[widest + 1:]
    return values.at[tuple(place)].set(low).at[tuple(next_to)].set(high)


def setup_inputs(seed: int = 0) -> dict:
    keys = jax.random.split(jax.random.key(seed), 8)
    return {
        "innovations": draw_innovations(jax.random.fold_in(keys[7], 71), 0),
        "obs_column": place_ends(jax.random.randint(keys[1], (NOBS,), 0, COLS_T), jax.random.fold_in(keys[1], 1), 0, COLS_T - 1).astype(jnp.int32),
        "obs_scale": draw_obs_scale(jax.random.fold_in(keys[7], 71), 0),
        "band_of_lat": draw_band_of_lat(jax.random.fold_in(keys[7], 71), 0),
        "balance": draw_balance(jax.random.fold_in(keys[7], 71), 0),
        "lon_filter": draw_lon_filter(jax.random.fold_in(keys[7], 71), 0),
        "lat_filter": draw_lat_filter(jax.random.fold_in(keys[7], 71), 0),
    }


huber_edge = 1.5


def rounded(value):
    return lax.optimization_barrier(value.astype(jnp.bfloat16)).astype(jnp.float32)


def reference(innovations, obs_column, obs_scale, band_of_lat, balance, lon_filter, lat_filter):
    tile_index = jnp.arange(NOBS, dtype=jnp.int32) // OBS_DEV
    lon_index = (tile_index // N_GY) * LON_T + obs_column // LAT_T
    lat_index = (tile_index % N_GY) * LAT_T + obs_column % LAT_T
    obs_site = (lon_index * NLAT + lat_index).astype(jnp.int32)
    balance_lat = balance[band_of_lat].astype(jnp.float32)
    lon_wide = lon_filter.astype(jnp.float32)
    lat_wide = lat_filter.astype(jnp.float32)
    inv_scale = obs_scale[:, :, None]
    grid_shape = (NVAR, NLEV, NLON, NLAT)
    control = jnp.zeros(grid_shape, jnp.float32)
    increment = jnp.zeros((NVAR, NLEV, NLON * NLAT), jnp.float32)
    for iteration in range(ITERS):
        observed = increment[:, :, obs_site]
        scaled = (observed - innovations) * inv_scale
        weighted = jnp.clip(scaled, -huber_edge, huber_edge) * inv_scale
        forcing = jnp.zeros((NVAR, NLEV, NLON * NLAT), jnp.float32).at[:, :, obs_site].add(weighted)
        forcing = rounded(forcing).reshape(grid_shape)
        balanced = rounded(jnp.einsum("tvlm,vlxt->vmxt", balance_lat, forcing))
        half_lon = rounded(jnp.einsum("vij,vlik->vljk", lon_wide, balanced))
        adjoint = jnp.einsum("vljm,vmk->vljk", half_lon, lat_wide)
        gradient = control + adjoint
        grad_norm = jnp.sum(gradient * gradient)
        grad_round = rounded(gradient)
        smooth_lon = rounded(jnp.einsum("vij,vljk->vlik", lon_wide, grad_round))
        smoothed = rounded(jnp.einsum("vlim,vkm->vlik", smooth_lon, lat_wide))
        response = jnp.einsum("tvlm,vmxt->vlxt", balance_lat, smoothed).reshape(NVAR, NLEV, NLON * NLAT)
        at_obs = response[:, :, obs_site]
        weight = huber_edge / jnp.maximum(jnp.abs(scaled), huber_edge)
        curvature = jnp.sum(weight * (inv_scale * at_obs) ** 2)
        step_size = grad_norm / (grad_norm + curvature)
        control = control - step_size * gradient
        increment = increment - step_size * response
    return control, increment.reshape(grid_shape)
```

```python
import jax
import jax.numpy as jnp
from jax import lax
from jax.sharding import PartitionSpec as P

ITERS = 2


huber_edge = 1.5


def split_bf16(values):
    high = lax.reduce_precision(values, exponent_bits=8, mantissa_bits=7)
    low = values - high
    return high.astype(jnp.bfloat16), low.astype(jnp.bfloat16)


def total_over(values, axes):
    count = lax.axis_size(axes)
    spread = jnp.broadcast_to(values[None, :], (count, values.shape[0]))
    return jnp.sum(lax.all_to_all(spread, axes, 0, 0, tiled=True), axis=0)


def filter_adjoint(pieces, lon_tiled, lat_tiled):
    half_lon = jnp.einsum(
        "vaxj,vablxt->vbljt", lon_tiled, pieces, preferred_element_type=jnp.float32
    ).astype(jnp.bfloat16)
    return jnp.einsum("vbljt,vbtk->vljk", half_lon, lat_tiled, preferred_element_type=jnp.float32)


def filter_forward(planes, lon_tiled, lat_tiled):
    smooth_lon = jnp.einsum(
        "vaxj,vljk->vlaxk", lon_tiled, planes, preferred_element_type=jnp.float32
    ).astype(jnp.bfloat16)
    return jnp.einsum(
        "vlaxm,vbtm->vablxt", smooth_lon, lat_tiled, preferred_element_type=jnp.float32
    ).astype(jnp.bfloat16)


def shards(innovations, obs_column, obs_scale, band_of_lat, balance, lon_filter, lat_filter):
    axes = ("gx", "gy")
    lon_parts = lax.axis_size("gx")
    lat_parts = lax.axis_size("gy")
    devices = lon_parts * lat_parts
    var_count, levels, obs_count = innovations.shape
    lon_full = lon_filter.shape[1]
    lat_full = lat_filter.shape[1]
    lon_tile = lon_full // lon_parts
    lat_tile = lat_full // lat_parts
    columns = lon_tile * lat_tile
    per_dev = levels // devices
    rows = var_count * levels
    lon_tiled = lon_filter.reshape(var_count, lon_parts, lon_tile, lon_full)
    lat_tiled = lat_filter.reshape(var_count, lat_parts, lat_tile, lat_full)
    inv_scale = obs_scale[:, :, None]
    scale_sq = inv_scale * inv_scale
    one_hot = (
        obs_column[:, None] == jnp.arange(columns, dtype=jnp.int32)[None, :]
    ).astype(jnp.bfloat16)
    band_hot = (
        band_of_lat[:, None] == jnp.arange(balance.shape[0], dtype=jnp.int32)[None, :]
    ).astype(jnp.bfloat16)
    balance_lat = jnp.einsum(
        "tb,bvlm->tvlm", band_hot, balance, preferred_element_type=jnp.float32
    ).astype(jnp.bfloat16)
    control = None
    increment = None
    for iteration in range(ITERS):
        if increment is None:
            scaled = -innovations * inv_scale
        else:
            inc_high, inc_low = split_bf16(increment.reshape(rows, columns))
            picked = lax.dot_general(
                jnp.concatenate([inc_high, inc_low], axis=0),
                one_hot,
                (((1,), (1,)), ((), ())),
                preferred_element_type=jnp.float32,
            )
            observed = (picked[:rows] + picked[rows:]).reshape(var_count, levels, obs_count)
            scaled = (observed - innovations) * inv_scale
        weighted = jnp.clip(scaled, -huber_edge, huber_edge) * inv_scale
        weight = huber_edge / jnp.maximum(jnp.abs(scaled), huber_edge)
        w_high, w_low = split_bf16(weighted.reshape(rows, obs_count))
        g_high, g_low = split_bf16(weight.reshape(rows, obs_count))
        sums = jnp.dot(
            jnp.concatenate([w_high, w_low, g_high, g_low], axis=0),
            one_hot,
            preferred_element_type=jnp.float32,
        )
        forcing = (sums[:rows] + sums[rows : 2 * rows]).astype(jnp.bfloat16)
        forcing = forcing.reshape(var_count, levels, lon_tile, lat_tile)
        obs_weight = (sums[2 * rows : 3 * rows] + sums[3 * rows :]).reshape(var_count, levels, columns)
        balanced = jnp.einsum(
            "tvlm,vlxt->vmxt", balance_lat, forcing, preferred_element_type=jnp.float32
        ).astype(jnp.bfloat16)
        pieces = lax.all_to_all(
            balanced.reshape(var_count, devices, per_dev, lon_tile, lat_tile),
            axes,
            split_axis=1,
            concat_axis=1,
            tiled=True,
        )
        item_count = pieces.shape[2]
        tiled = pieces.reshape(var_count, lon_parts, lat_parts, item_count, lon_tile, lat_tile)
        adjoint = filter_adjoint(tiled, lon_tiled, lat_tiled)
        gradient = adjoint if control is None else control + adjoint
        grad_local = jnp.sum(gradient * gradient)
        smoothed = filter_forward(gradient.astype(jnp.bfloat16), lon_tiled, lat_tiled)
        outgoing = smoothed.reshape(var_count, devices, per_dev, lon_tile, lat_tile)
        returned = lax.all_to_all(outgoing, axes, split_axis=1, concat_axis=1, tiled=True)
        returned = returned.reshape(var_count, levels, lon_tile, lat_tile)
        response = jnp.einsum(
            "tvlm,vmxt->vlxt", balance_lat, returned, preferred_element_type=jnp.float32
        )
        response = response.reshape(var_count, levels, columns)
        curve_local = jnp.sum(scale_sq * obs_weight * response * response)
        totals = total_over(jnp.stack([grad_local, curve_local]), axes)
        grad_norm = totals[0]
        curvature = totals[1]
        step_size = grad_norm / (grad_norm + curvature)
        if control is None:
            control = -(step_size * gradient)
            increment = -(step_size * response)
        else:
            control = control - step_size * gradient
            increment = increment - step_size * response
    return (control, increment.reshape(var_count, levels, lon_tile, lat_tile))


def solution(mesh):
    in_specs = (P(None, None, ("gx", "gy")), P(("gx", "gy")), P(), P("gy"), P(), P(), P())
    out_specs = (P(None, ("gx", "gy"), None, None), P(None, None, "gx", "gy"))
    return jax.shard_map(shards, mesh=mesh, in_specs=in_specs, out_specs=out_specs, check_vma=False)
```

```python
import jax
import jax.numpy as jnp
from jax import lax
from jax.sharding import PartitionSpec as P

ITERS = 2


huber_edge = 1.5


def split_bf16(values):
    high = lax.reduce_precision(values, exponent_bits=8, mantissa_bits=7)
    low = values - high
    return high.astype(jnp.bfloat16), low.astype(jnp.bfloat16)


def total_over(values, axes):
    count = lax.axis_size(axes)
    spread = jnp.broadcast_to(values[None, :], (count, values.shape[0]))
    return jnp.sum(lax.all_to_all(spread, axes, 0, 0, tiled=True), axis=0)


def filter_adjoint(pieces, lon_tiled, lat_tiled):
    half_lon = jnp.einsum(
        "vaxj,vablxt->vbljt", lon_tiled, pieces, preferred_element_type=jnp.float32
    ).astype(jnp.bfloat16)
    return jnp.einsum("vbljt,vbtk->vljk", half_lon, lat_tiled, preferred_element_type=jnp.float32)


def filter_forward(planes, lon_tiled, lat_tiled):
    smooth_lon = jnp.einsum(
        "vaxj,vljk->vlaxk", lon_tiled, planes, preferred_element_type=jnp.float32
    ).astype(jnp.bfloat16)
    return jnp.einsum(
        "vlaxm,vbtm->vablxt", smooth_lon, lat_tiled, preferred_element_type=jnp.float32
    ).astype(jnp.bfloat16)


def shards(innovations, obs_column, obs_scale, band_of_lat, balance, lon_filter, lat_filter):
    axes = ("gx", "gy")
    lon_parts = lax.axis_size("gx")
    lat_parts = lax.axis_size("gy")
    devices = lon_parts * lat_parts
    var_count, levels, obs_count = innovations.shape
    lon_full = lon_filter.shape[1]
    lat_full = lat_filter.shape[1]
    lon_tile = lon_full // lon_parts
    lat_tile = lat_full // lat_parts
    columns = lon_tile * lat_tile
    per_dev = levels // devices
    rows = var_count * levels
    lon_tiled = lon_filter.reshape(var_count, lon_parts, lon_tile, lon_full)
    lat_tiled = lat_filter.reshape(var_count, lat_parts, lat_tile, lat_full)
    inv_scale = obs_scale[:, :, None]
    one_hot = (
        obs_column[:, None] == jnp.arange(columns, dtype=jnp.int32)[None, :]
    ).astype(jnp.bfloat16)
    band_hot = (
        band_of_lat[:, None] == jnp.arange(balance.shape[0], dtype=jnp.int32)[None, :]
    ).astype(jnp.bfloat16)
    balance_lat = jnp.einsum(
        "tb,bvlm->tvlm", band_hot, balance, preferred_element_type=jnp.float32
    ).astype(jnp.bfloat16)
    one_hot_pair = jnp.concatenate([one_hot, one_hot], axis=0)
    one_hot_grid = one_hot.reshape(obs_count, lon_tile, lat_tile)
    control = None
    increment = None
    inc_obs = None
    for iteration in range(ITERS):
        if inc_obs is None:
            scaled = -innovations * inv_scale
        else:
            scaled = (inc_obs - innovations) * inv_scale
        weighted = jnp.clip(scaled, -huber_edge, huber_edge) * inv_scale
        w_high, w_low = split_bf16(weighted.reshape(rows, obs_count))
        forcing = jnp.dot(
            jnp.concatenate([w_high, w_low], axis=1),
            one_hot_pair,
            preferred_element_type=jnp.float32,
        ).astype(jnp.bfloat16)
        forcing = forcing.reshape(var_count, levels, lon_tile, lat_tile)
        balanced = jnp.einsum(
            "tvlm,vlxt->vmxt", balance_lat, forcing, preferred_element_type=jnp.float32
        ).astype(jnp.bfloat16)
        pieces = lax.all_to_all(
            balanced.reshape(var_count, devices, per_dev, lon_tile, lat_tile),
            axes,
            split_axis=1,
            concat_axis=1,
            tiled=True,
        )
        item_count = pieces.shape[2]
        tiled = pieces.reshape(var_count, lon_parts, lat_parts, item_count, lon_tile, lat_tile)
        adjoint = filter_adjoint(tiled, lon_tiled, lat_tiled)
        gradient = adjoint if control is None else control + adjoint
        grad_local = jnp.sum(gradient * gradient)
        smoothed = filter_forward(gradient.astype(jnp.bfloat16), lon_tiled, lat_tiled)
        outgoing = smoothed.reshape(var_count, devices, per_dev, lon_tile, lat_tile)
        returned = lax.all_to_all(outgoing, axes, split_axis=1, concat_axis=1, tiled=True)
        returned = returned.reshape(var_count, levels, lon_tile, lat_tile)
        response = jnp.einsum(
            "tvlm,vmxt->vlxt", balance_lat, returned, preferred_element_type=jnp.float32
        )
        r_high, r_low = split_bf16(response)
        at_obs = jnp.einsum(
            "vlxt,jxt->vlj", r_high, one_hot_grid, preferred_element_type=jnp.float32
        ) + jnp.einsum("vlxt,jxt->vlj", r_low, one_hot_grid, preferred_element_type=jnp.float32)
        weight = huber_edge / jnp.maximum(jnp.abs(scaled), huber_edge)
        curve_local = jnp.sum(weight * (inv_scale * at_obs) ** 2)
        totals = total_over(jnp.stack([grad_local, curve_local]), axes)
        grad_norm = totals[0]
        curvature = totals[1]
        step_size = grad_norm / (grad_norm + curvature)
        if control is None:
            control = -(step_size * gradient)
            increment = -(step_size * response)
            inc_obs = -(step_size * at_obs)
        else:
            control = control - step_size * gradient
            increment = increment - step_size * response
            inc_obs = inc_obs - step_size * at_obs
    return (control, increment)


def solution(mesh):
    in_specs = (P(None, None, ("gx", "gy")), P(("gx", "gy")), P(), P("gy"), P(), P(), P())
    out_specs = (P(None, ("gx", "gy"), None, None), P(None, None, "gx", "gy"))
    return jax.shard_map(shards, mesh=mesh, in_specs=in_specs, out_specs=out_specs, check_vma=False)
```

```python
import jax
import jax.numpy as jnp
from jax import lax
from jax.sharding import PartitionSpec as P

ITERS = 2


huber_edge = 1.5


def split_bf16(values):
    high = lax.reduce_precision(values, exponent_bits=8, mantissa_bits=7)
    low = values - high
    return high.astype(jnp.bfloat16), low.astype(jnp.bfloat16)


def total_over(values, axes):
    count = lax.axis_size(axes)
    spread = jnp.broadcast_to(values[None, :], (count, values.shape[0]))
    return jnp.sum(lax.all_to_all(spread, axes, 0, 0, tiled=True), axis=0)


def filter_adjoint(pieces, lon_tiled, lat_tiled):
    half_lon = jnp.einsum(
        "vaxj,vablxt->vbljt", lon_tiled, pieces, preferred_element_type=jnp.float32
    ).astype(jnp.bfloat16)
    return jnp.einsum("vbljt,vbtk->vljk", half_lon, lat_tiled, preferred_element_type=jnp.float32)


def filter_forward(planes, lon_tiled, lat_tiled):
    smooth_lon = jnp.einsum(
        "vaxj,vljk->vlaxk", lon_tiled, planes, preferred_element_type=jnp.float32
    ).astype(jnp.bfloat16)
    return jnp.einsum(
        "vlaxm,vbtm->vablxt", smooth_lon, lat_tiled, preferred_element_type=jnp.float32
    ).astype(jnp.bfloat16)


def shards(innovations, obs_column, obs_scale, band_of_lat, balance, lon_filter, lat_filter):
    axes = ("gx", "gy")
    lon_parts = lax.axis_size("gx")
    lat_parts = lax.axis_size("gy")
    devices = lon_parts * lat_parts
    var_count, levels, obs_count = innovations.shape
    lon_full = lon_filter.shape[1]
    lat_full = lat_filter.shape[1]
    lon_tile = lon_full // lon_parts
    lat_tile = lat_full // lat_parts
    columns = lon_tile * lat_tile
    per_dev = levels // devices
    rows = var_count * levels
    lon_tiled = lon_filter.reshape(var_count, lon_parts, lon_tile, lon_full)
    lat_tiled = lat_filter.reshape(var_count, lat_parts, lat_tile, lat_full)
    inv_scale = obs_scale[:, :, None]
    one_hot = (
        obs_column[:, None] == jnp.arange(columns, dtype=jnp.int32)[None, :]
    ).astype(jnp.bfloat16)
    band_hot = (
        band_of_lat[:, None] == jnp.arange(balance.shape[0], dtype=jnp.int32)[None, :]
    ).astype(jnp.bfloat16)
    balance_lat = jnp.einsum(
        "tb,bvlm->tvlm", band_hot, balance, preferred_element_type=jnp.float32
    ).astype(jnp.bfloat16)
    one_hot_pair = jnp.concatenate([one_hot, one_hot], axis=0)
    one_hot_grid = one_hot.reshape(obs_count, lon_tile, lat_tile)
    control = None
    increment = None
    inc_obs = None
    for iteration in range(ITERS):
        if inc_obs is None:
            scaled = -innovations * inv_scale
        else:
            scaled = (inc_obs - innovations) * inv_scale
        weighted = jnp.clip(scaled, -huber_edge, huber_edge) * inv_scale
        w_high, w_low = split_bf16(weighted.reshape(rows, obs_count))
        forcing = jnp.dot(
            jnp.concatenate([w_high, w_low], axis=1),
            one_hot_pair,
            preferred_element_type=jnp.float32,
        ).astype(jnp.bfloat16)
        forcing = forcing.reshape(var_count, levels, lon_tile, lat_tile)
        grad_parts = []
        gradients = []
        responses = []
        obs_parts = []
        for var in range(var_count):
            balanced = jnp.einsum(
                "tlm,lxt->mxt", balance_lat[:, var], forcing[var], preferred_element_type=jnp.float32
            ).astype(jnp.bfloat16)
            pieces = lax.all_to_all(
                balanced.reshape(devices, per_dev, lon_tile, lat_tile), axes, 0, 0, tiled=True
            )
            tiled = pieces.reshape(lon_parts, lat_parts, per_dev, lon_tile, lat_tile)
            half_lon = jnp.einsum(
                "axj,ablxt->bljt", lon_tiled[var], tiled, preferred_element_type=jnp.float32
            ).astype(jnp.bfloat16)
            adjoint = jnp.einsum("bljt,btk->ljk", half_lon, lat_tiled[var], preferred_element_type=jnp.float32)
            gradient = adjoint if control is None else control[var] + adjoint
            grad_parts.append(jnp.sum(gradient * gradient))
            gradients.append(gradient)
            smooth_lon = jnp.einsum(
                "axj,ljk->laxk", lon_tiled[var], gradient.astype(jnp.bfloat16), preferred_element_type=jnp.float32
            ).astype(jnp.bfloat16)
            smoothed = jnp.einsum(
                "laxm,btm->ablxt", smooth_lon, lat_tiled[var], preferred_element_type=jnp.float32
            ).astype(jnp.bfloat16)
            returned = lax.all_to_all(
                smoothed.reshape(devices, per_dev, lon_tile, lat_tile), axes, 0, 0, tiled=True
            ).reshape(levels, lon_tile, lat_tile)
            response = jnp.einsum(
                "tlm,mxt->lxt", balance_lat[:, var], returned, preferred_element_type=jnp.float32
            )
            responses.append(response)
            r_high, r_low = split_bf16(response)
            obs_parts.append(
                jnp.einsum("lxt,jxt->lj", r_high, one_hot_grid, preferred_element_type=jnp.float32)
                + jnp.einsum("lxt,jxt->lj", r_low, one_hot_grid, preferred_element_type=jnp.float32)
            )
        gradient = jnp.stack(gradients)
        response = jnp.stack(responses)
        at_obs = jnp.stack(obs_parts)
        grad_local = sum(grad_parts)
        weight = huber_edge / jnp.maximum(jnp.abs(scaled), huber_edge)
        curve_local = jnp.sum(weight * (inv_scale * at_obs) ** 2)
        totals = total_over(jnp.stack([grad_local, curve_local]), axes)
        grad_norm = totals[0]
        curvature = totals[1]
        step_size = grad_norm / (grad_norm + curvature)
        if control is None:
            control = -(step_size * gradient)
            increment = -(step_size * response)
            inc_obs = -(step_size * at_obs)
        else:
            control = control - step_size * gradient
            increment = increment - step_size * response
            inc_obs = inc_obs - step_size * at_obs
    return (control, increment)


def solution(mesh):
    in_specs = (P(None, None, ("gx", "gy")), P(("gx", "gy")), P(), P("gy"), P(), P(), P())
    out_specs = (P(None, ("gx", "gy"), None, None), P(None, None, "gx", "gy"))
    return jax.shard_map(shards, mesh=mesh, in_specs=in_specs, out_specs=out_specs, check_vma=False)
```

```python
import jax
import jax.numpy as jnp
from jax import lax
from jax.sharding import PartitionSpec as P

ITERS = 2


huber_edge = 1.5


def split_bf16(values):
    high = lax.reduce_precision(values, exponent_bits=8, mantissa_bits=7)
    low = values - high
    return high.astype(jnp.bfloat16), low.astype(jnp.bfloat16)


def total_over(values, axes):
    count = lax.axis_size(axes)
    spread = jnp.broadcast_to(values[None, :], (count, values.shape[0]))
    return jnp.sum(lax.all_to_all(spread, axes, 0, 0, tiled=True), axis=0)


def filter_adjoint(pieces, lon_tiled, lat_tiled):
    half_lon = jnp.einsum(
        "vaxj,vablxt->vbljt", lon_tiled, pieces, preferred_element_type=jnp.float32
    ).astype(jnp.bfloat16)
    return jnp.einsum("vbljt,vbtk->vljk", half_lon, lat_tiled, preferred_element_type=jnp.float32)


def filter_forward(planes, lon_tiled, lat_tiled):
    smooth_lon = jnp.einsum(
        "vaxj,vljk->vlaxk", lon_tiled, planes, preferred_element_type=jnp.float32
    ).astype(jnp.bfloat16)
    return jnp.einsum(
        "vlaxm,vbtm->vablxt", smooth_lon, lat_tiled, preferred_element_type=jnp.float32
    ).astype(jnp.bfloat16)


def shards(innovations, obs_column, obs_scale, band_of_lat, balance, lon_filter, lat_filter):
    axes = ("gx", "gy")
    lon_parts = lax.axis_size("gx")
    lat_parts = lax.axis_size("gy")
    devices = lon_parts * lat_parts
    var_count, levels, obs_count = innovations.shape
    lon_full = lon_filter.shape[1]
    lat_full = lat_filter.shape[1]
    lon_tile = lon_full // lon_parts
    lat_tile = lat_full // lat_parts
    columns = lon_tile * lat_tile
    per_dev = levels // devices
    rows = var_count * levels
    lon_tiled = lon_filter.reshape(var_count, lon_parts, lon_tile, lon_full)
    lat_tiled = lat_filter.reshape(var_count, lat_parts, lat_tile, lat_full)
    inv_scale = obs_scale[:, :, None]
    one_hot = (
        obs_column[:, None] == jnp.arange(columns, dtype=jnp.int32)[None, :]
    ).astype(jnp.bfloat16)
    bands = balance.shape[0]
    lat_of_column = jnp.arange(columns, dtype=jnp.int32) % lat_tile
    band_mask = (
        band_of_lat[lat_of_column][None, :] == jnp.arange(bands, dtype=jnp.int32)[:, None]
    ).astype(jnp.bfloat16)
    balance_adj = jnp.transpose(balance, (1, 3, 0, 2)).reshape(var_count, levels, bands * levels)
    balance_fwd = jnp.transpose(balance, (1, 2, 0, 3)).reshape(var_count, levels, bands * levels)
    one_hot_pair = jnp.concatenate([one_hot, one_hot], axis=0)
    control = None
    increment = None
    inc_obs = None
    for iteration in range(ITERS):
        if inc_obs is None:
            scaled = -innovations * inv_scale
        else:
            scaled = (inc_obs - innovations) * inv_scale
        weighted = jnp.clip(scaled, -huber_edge, huber_edge) * inv_scale
        w_high, w_low = split_bf16(weighted.reshape(rows, obs_count))
        forcing = jnp.dot(
            jnp.concatenate([w_high, w_low], axis=1),
            one_hot_pair,
            preferred_element_type=jnp.float32,
        ).astype(jnp.bfloat16)
        forcing = forcing.reshape(var_count, levels, columns)
        grad_parts = []
        gradients = []
        responses = []
        obs_parts = []
        for var in range(var_count):
            banded = (band_mask[:, None, :] * forcing[var][None, :, :]).reshape(bands * levels, columns)
            balanced = jnp.dot(
                balance_adj[var], banded, preferred_element_type=jnp.float32
            ).astype(jnp.bfloat16)
            pieces = lax.all_to_all(
                balanced.reshape(devices, per_dev, lon_tile, lat_tile), axes, 0, 0, tiled=True
            )
            tiled = pieces.reshape(lon_parts, lat_parts, per_dev, lon_tile, lat_tile)
            half_lon = jnp.einsum(
                "axj,ablxt->bljt", lon_tiled[var], tiled, preferred_element_type=jnp.float32
            ).astype(jnp.bfloat16)
            adjoint = jnp.einsum("bljt,btk->ljk", half_lon, lat_tiled[var], preferred_element_type=jnp.float32)
            gradient = adjoint if control is None else control[var] + adjoint
            grad_parts.append(jnp.sum(gradient * gradient))
            gradients.append(gradient)
            smooth_lon = jnp.einsum(
                "axj,ljk->laxk", lon_tiled[var], gradient.astype(jnp.bfloat16), preferred_element_type=jnp.float32
            ).astype(jnp.bfloat16)
            smoothed = jnp.einsum(
                "laxm,btm->ablxt", smooth_lon, lat_tiled[var], preferred_element_type=jnp.float32
            ).astype(jnp.bfloat16)
            returned = lax.all_to_all(
                smoothed.reshape(devices, per_dev, lon_tile, lat_tile), axes, 0, 0, tiled=True
            ).reshape(levels, columns)
            banded = (band_mask[:, None, :] * returned[None, :, :]).reshape(bands * levels, columns)
            response = jnp.dot(balance_fwd[var], banded, preferred_element_type=jnp.float32)
            responses.append(response)
            r_high, r_low = split_bf16(response)
            obs_parts.append(
                jnp.einsum("lc,jc->lj", r_high, one_hot, preferred_element_type=jnp.float32)
                + jnp.einsum("lc,jc->lj", r_low, one_hot, preferred_element_type=jnp.float32)
            )
        gradient = jnp.stack(gradients)
        response = jnp.stack(responses)
        at_obs = jnp.stack(obs_parts)
        grad_local = sum(grad_parts)
        weight = huber_edge / jnp.maximum(jnp.abs(scaled), huber_edge)
        curve_local = jnp.sum(weight * (inv_scale * at_obs) ** 2)
        totals = total_over(jnp.stack([grad_local, curve_local]), axes)
        grad_norm = totals[0]
        curvature = totals[1]
        step_size = grad_norm / (grad_norm + curvature)
        if control is None:
            control = -(step_size * gradient)
            increment = -(step_size * response)
            inc_obs = -(step_size * at_obs)
        else:
            control = control - step_size * gradient
            increment = increment - step_size * response
            inc_obs = inc_obs - step_size * at_obs
    return (control, increment.reshape(var_count, levels, lon_tile, lat_tile))


def solution(mesh):
    in_specs = (P(None, None, ("gx", "gy")), P(("gx", "gy")), P(), P("gy"), P(), P(), P())
    out_specs = (P(None, ("gx", "gy"), None, None), P(None, None, "gx", "gy"))
    return jax.shard_map(shards, mesh=mesh, in_specs=in_specs, out_specs=out_specs, check_vma=False)
```

```python
import jax
import jax.numpy as jnp
from jax import lax
from jax.sharding import PartitionSpec as P
from jax.experimental import pallas as pl

ITERS = 2


huber_edge = 1.5


def _band_mix_kernel(mat_ref, rhs_ref, mask_ref, out_ref):
    rhs = rhs_ref[...]
    acc = jnp.zeros(out_ref.shape, jnp.float32)
    for band in range(mat_ref.shape[0]):
        masked = rhs * mask_ref[band : band + 1, :]
        acc = acc + jnp.dot(mat_ref[band], masked, preferred_element_type=jnp.float32)
    out_ref[...] = acc.astype(out_ref.dtype)


def band_mix(mats, rhs, mask, out_dtype, block=1024):
    bands, rows, inner = mats.shape
    columns = rhs.shape[1]
    return pl.pallas_call(
        _band_mix_kernel,
        grid=(columns // block,),
        in_specs=[
            pl.BlockSpec((bands, rows, inner), lambda i: (0, 0, 0)),
            pl.BlockSpec((inner, block), lambda i: (0, i)),
            pl.BlockSpec((bands, block), lambda i: (0, i)),
        ],
        out_specs=pl.BlockSpec((rows, block), lambda i: (0, i)),
        out_shape=jax.ShapeDtypeStruct((rows, columns), out_dtype),
    )(mats, rhs, mask)


def split_bf16(values):
    high = lax.reduce_precision(values, exponent_bits=8, mantissa_bits=7)
    low = values - high
    return high.astype(jnp.bfloat16), low.astype(jnp.bfloat16)


def total_over(values, axes):
    count = lax.axis_size(axes)
    spread = jnp.broadcast_to(values[None, :], (count, values.shape[0]))
    return jnp.sum(lax.all_to_all(spread, axes, 0, 0, tiled=True), axis=0)


def filter_adjoint(pieces, lon_tiled, lat_tiled):
    half_lon = jnp.einsum(
        "vaxj,vablxt->vbljt", lon_tiled, pieces, preferred_element_type=jnp.float32
    ).astype(jnp.bfloat16)
    return jnp.einsum("vbljt,vbtk->vljk", half_lon, lat_tiled, preferred_element_type=jnp.float32)


def filter_forward(planes, lon_tiled, lat_tiled):
    smooth_lon = jnp.einsum(
        "vaxj,vljk->vlaxk", lon_tiled, planes, preferred_element_type=jnp.float32
    ).astype(jnp.bfloat16)
    return jnp.einsum(
        "vlaxm,vbtm->vablxt", smooth_lon, lat_tiled, preferred_element_type=jnp.float32
    ).astype(jnp.bfloat16)


def shards(innovations, obs_column, obs_scale, band_of_lat, balance, lon_filter, lat_filter):
    axes = ("gx", "gy")
    lon_parts = lax.axis_size("gx")
    lat_parts = lax.axis_size("gy")
    devices = lon_parts * lat_parts
    var_count, levels, obs_count = innovations.shape
    lon_full = lon_filter.shape[1]
    lat_full = lat_filter.shape[1]
    lon_tile = lon_full // lon_parts
    lat_tile = lat_full // lat_parts
    columns = lon_tile * lat_tile
    per_dev = levels // devices
    rows = var_count * levels
    lon_tiled = lon_filter.reshape(var_count, lon_parts, lon_tile, lon_full)
    lat_tiled = lat_filter.reshape(var_count, lat_parts, lat_tile, lat_full)
    inv_scale = obs_scale[:, :, None]
    one_hot = (
        obs_column[:, None] == jnp.arange(columns, dtype=jnp.int32)[None, :]
    ).astype(jnp.bfloat16)
    bands = balance.shape[0]
    band_hot = (
        band_of_lat[None, :] == jnp.arange(bands, dtype=jnp.int32)[:, None]
    ).astype(jnp.bfloat16)
    band_mask = jnp.broadcast_to(band_hot[:, None, :], (bands, lon_tile, lat_tile)).reshape(bands, columns)
    balance_adj = jnp.transpose(balance, (1, 0, 3, 2))
    balance_fwd = jnp.transpose(balance, (1, 0, 2, 3))
    one_hot_pair = jnp.concatenate([one_hot, one_hot], axis=0)
    control = None
    increment = None
    inc_obs = None
    for iteration in range(ITERS):
        if inc_obs is None:
            scaled = -innovations * inv_scale
        else:
            scaled = (inc_obs - innovations) * inv_scale
        weighted = jnp.clip(scaled, -huber_edge, huber_edge) * inv_scale
        w_high, w_low = split_bf16(weighted.reshape(rows, obs_count))
        forcing = jnp.dot(
            jnp.concatenate([w_high, w_low], axis=1),
            one_hot_pair,
            preferred_element_type=jnp.float32,
        ).astype(jnp.bfloat16)
        forcing = forcing.reshape(var_count, levels, columns)
        grad_parts = []
        gradients = []
        responses = []
        obs_parts = []
        for var in range(var_count):
            balanced = band_mix(balance_adj[var], forcing[var], band_mask, jnp.bfloat16)
            pieces = lax.all_to_all(
                balanced.reshape(devices, 2, per_dev * columns // 2), axes, 0, 0, tiled=True
            )
            tiled = pieces.reshape(lon_parts, lat_parts, per_dev, lon_tile, lat_tile)
            half_lon = jnp.einsum(
                "axj,ablxt->bljt", lon_tiled[var], tiled, preferred_element_type=jnp.float32
            ).astype(jnp.bfloat16)
            adjoint = jnp.einsum("bljt,btk->ljk", half_lon, lat_tiled[var], preferred_element_type=jnp.float32)
            gradient = adjoint if control is None else control[var] + adjoint
            grad_parts.append(jnp.sum(gradient * gradient))
            gradients.append(gradient)
            smooth_lon = jnp.einsum(
                "axj,ljk->laxk", lon_tiled[var], gradient.astype(jnp.bfloat16), preferred_element_type=jnp.float32
            ).astype(jnp.bfloat16)
            smoothed = jnp.einsum(
                "laxm,btm->ablxt", smooth_lon, lat_tiled[var], preferred_element_type=jnp.float32
            ).astype(jnp.bfloat16)
            returned = lax.all_to_all(
                smoothed.reshape(devices, 2, per_dev * columns // 2), axes, 0, 0, tiled=True
            ).reshape(levels, columns)
            response = band_mix(balance_fwd[var], returned, band_mask, jnp.float32)
            responses.append(response)
            r_high, r_low = split_bf16(response)
            obs_parts.append(
                jnp.einsum("lc,jc->lj", r_high, one_hot, preferred_element_type=jnp.float32)
                + jnp.einsum("lc,jc->lj", r_low, one_hot, preferred_element_type=jnp.float32)
            )
        gradient = jnp.stack(gradients)
        response = jnp.stack(responses)
        at_obs = jnp.stack(obs_parts)
        grad_local = sum(grad_parts)
        weight = huber_edge / jnp.maximum(jnp.abs(scaled), huber_edge)
        curve_local = jnp.sum(weight * (inv_scale * at_obs) ** 2)
        totals = total_over(jnp.stack([grad_local, curve_local]), axes)
        grad_norm = totals[0]
        curvature = totals[1]
        step_size = grad_norm / (grad_norm + curvature)
        if control is None:
            control = -(step_size * gradient)
            increment = -(step_size * response)
            inc_obs = -(step_size * at_obs)
        else:
            control = control - step_size * gradient
            increment = increment - step_size * response
            inc_obs = inc_obs - step_size * at_obs
    return (control, increment.reshape(var_count, levels, lon_tile, lat_tile))


def solution(mesh):
    in_specs = (P(None, None, ("gx", "gy")), P(("gx", "gy")), P(), P("gy"), P(), P(), P())
    out_specs = (P(None, ("gx", "gy"), None, None), P(None, None, "gx", "gy"))
    return jax.shard_map(shards, mesh=mesh, in_specs=in_specs, out_specs=out_specs, check_vma=False)
```

```python
import jax
import jax.numpy as jnp
from jax import lax
from jax.sharding import PartitionSpec as P
from jax.experimental import pallas as pl
from jax.experimental.pallas import tpu as pltpu

ITERS = 2


huber_edge = 1.5


def _band_mix_kernel(present_ref, mat_ref, rhs_ref, mask_ref, out_ref, acc_ref):
    acc_ref[...] = jnp.zeros(acc_ref.shape, jnp.float32)
    for band in range(mat_ref.shape[0]):

        @pl.when(present_ref[band] > 0)
        def _():
            masked = rhs_ref[...] * mask_ref[band : band + 1, :]
            acc_ref[...] += jnp.dot(mat_ref[band], masked, preferred_element_type=jnp.float32)

    out_ref[...] = acc_ref[...].astype(out_ref.dtype)


def band_mix(present, mats, rhs, mask, out_dtype, block=1024):
    bands, rows, inner = mats.shape
    columns = rhs.shape[1]
    return pl.pallas_call(
        _band_mix_kernel,
        grid_spec=pltpu.PrefetchScalarGridSpec(
            num_scalar_prefetch=1,
            grid=(columns // block,),
            in_specs=[
                pl.BlockSpec((bands, rows, inner), lambda i, p: (0, 0, 0)),
                pl.BlockSpec((inner, block), lambda i, p: (0, i)),
                pl.BlockSpec((bands, block), lambda i, p: (0, i)),
            ],
            out_specs=pl.BlockSpec((rows, block), lambda i, p: (0, i)),
            scratch_shapes=[pltpu.VMEM((rows, block), jnp.float32)],
        ),
        out_shape=jax.ShapeDtypeStruct((rows, columns), out_dtype),
    )(present, mats, rhs, mask)


def split_bf16(values):
    high = lax.reduce_precision(values, exponent_bits=8, mantissa_bits=7)
    low = values - high
    return high.astype(jnp.bfloat16), low.astype(jnp.bfloat16)


def total_over(values, axes):
    count = lax.axis_size(axes)
    spread = jnp.broadcast_to(values[None, :], (count, values.shape[0]))
    return jnp.sum(lax.all_to_all(spread, axes, 0, 0, tiled=True), axis=0)


def filter_adjoint(pieces, lon_tiled, lat_tiled):
    half_lon = jnp.einsum(
        "vaxj,vablxt->vbljt", lon_tiled, pieces, preferred_element_type=jnp.float32
    ).astype(jnp.bfloat16)
    return jnp.einsum("vbljt,vbtk->vljk", half_lon, lat_tiled, preferred_element_type=jnp.float32)


def filter_forward(planes, lon_tiled, lat_tiled):
    smooth_lon = jnp.einsum(
        "vaxj,vljk->vlaxk", lon_tiled, planes, preferred_element_type=jnp.float32
    ).astype(jnp.bfloat16)
    return jnp.einsum(
        "vlaxm,vbtm->vablxt", smooth_lon, lat_tiled, preferred_element_type=jnp.float32
    ).astype(jnp.bfloat16)


def shards(innovations, obs_column, obs_scale, band_of_lat, balance, lon_filter, lat_filter):
    axes = ("gx", "gy")
    lon_parts = lax.axis_size("gx")
    lat_parts = lax.axis_size("gy")
    devices = lon_parts * lat_parts
    var_count, levels, obs_count = innovations.shape
    lon_full = lon_filter.shape[1]
    lat_full = lat_filter.shape[1]
    lon_tile = lon_full // lon_parts
    lat_tile = lat_full // lat_parts
    columns = lon_tile * lat_tile
    per_dev = levels // devices
    rows = var_count * levels
    lon_tiled = lon_filter.reshape(var_count, lon_parts, lon_tile, lon_full)
    lat_tiled = lat_filter.reshape(var_count, lat_parts, lat_tile, lat_full)
    inv_scale = obs_scale[:, :, None]
    one_hot = (
        obs_column[:, None] == jnp.arange(columns, dtype=jnp.int32)[None, :]
    ).astype(jnp.bfloat16)
    bands = balance.shape[0]
    band_hot = (
        band_of_lat[None, :] == jnp.arange(bands, dtype=jnp.int32)[:, None]
    ).astype(jnp.bfloat16)
    band_present = jnp.max(band_hot, axis=1).astype(jnp.int32)
    band_mask = jnp.broadcast_to(band_hot[:, None, :], (bands, lon_tile, lat_tile)).reshape(bands, columns)
    balance_adj = jnp.transpose(balance, (1, 0, 3, 2))
    balance_fwd = jnp.transpose(balance, (1, 0, 2, 3))
    one_hot_pair = jnp.concatenate([one_hot, one_hot], axis=0)
    control = None
    increment = None
    inc_obs = None
    for iteration in range(ITERS):
        if inc_obs is None:
            scaled = -innovations * inv_scale
        else:
            scaled = (inc_obs - innovations) * inv_scale
        weighted = jnp.clip(scaled, -huber_edge, huber_edge) * inv_scale
        w_high, w_low = split_bf16(weighted.reshape(rows, obs_count))
        forcing = jnp.dot(
            jnp.concatenate([w_high, w_low], axis=1),
            one_hot_pair,
            preferred_element_type=jnp.float32,
        ).astype(jnp.bfloat16)
        forcing = forcing.reshape(var_count, levels, columns)
        grad_parts = []
        gradients = []
        responses = []
        obs_parts = []
        for var in range(var_count):
            balanced = band_mix(band_present, balance_adj[var], forcing[var], band_mask, jnp.bfloat16)
            pieces = lax.all_to_all(
                balanced.reshape(devices, 2, per_dev * columns // 2), axes, 0, 0, tiled=True
            )
            tiled = pieces.reshape(lon_parts, lat_parts, per_dev, lon_tile, lat_tile)
            half_lon = jnp.einsum(
                "axj,ablxt->bljt", lon_tiled[var], tiled, preferred_element_type=jnp.float32
            ).astype(jnp.bfloat16)
            adjoint = jnp.einsum("bljt,btk->ljk", half_lon, lat_tiled[var], preferred_element_type=jnp.float32)
            gradient = adjoint if control is None else control[var] + adjoint
            grad_parts.append(jnp.sum(gradient * gradient))
            gradients.append(gradient)
            smooth_lon = jnp.einsum(
                "axj,ljk->laxk", lon_tiled[var], gradient.astype(jnp.bfloat16), preferred_element_type=jnp.float32
            ).astype(jnp.bfloat16)
            smoothed = jnp.einsum(
                "laxm,btm->ablxt", smooth_lon, lat_tiled[var], preferred_element_type=jnp.float32
            ).astype(jnp.bfloat16)
            returned = lax.all_to_all(
                smoothed.reshape(devices, 2, per_dev * columns // 2), axes, 0, 0, tiled=True
            ).reshape(levels, columns)
            response = band_mix(band_present, balance_fwd[var], returned, band_mask, jnp.float32)
            responses.append(response)
            r_high, r_low = split_bf16(response)
            obs_parts.append(
                jnp.einsum("lc,jc->lj", r_high, one_hot, preferred_element_type=jnp.float32)
                + jnp.einsum("lc,jc->lj", r_low, one_hot, preferred_element_type=jnp.float32)
            )
        gradient = jnp.stack(gradients)
        response = jnp.stack(responses)
        at_obs = jnp.stack(obs_parts)
        grad_local = sum(grad_parts)
        weight = huber_edge / jnp.maximum(jnp.abs(scaled), huber_edge)
        curve_local = jnp.sum(weight * (inv_scale * at_obs) ** 2)
        totals = total_over(jnp.stack([grad_local, curve_local]), axes)
        grad_norm = totals[0]
        curvature = totals[1]
        step_size = grad_norm / (grad_norm + curvature)
        if control is None:
            control = -(step_size * gradient)
            increment = -(step_size * response)
            inc_obs = -(step_size * at_obs)
        else:
            control = control - step_size * gradient
            increment = increment - step_size * response
            inc_obs = inc_obs - step_size * at_obs
    return (control, increment.reshape(var_count, levels, lon_tile, lat_tile))


def solution(mesh):
    in_specs = (P(None, None, ("gx", "gy")), P(("gx", "gy")), P(), P("gy"), P(), P(), P())
    out_specs = (P(None, ("gx", "gy"), None, None), P(None, None, "gx", "gy"))
    return jax.shard_map(shards, mesh=mesh, in_specs=in_specs, out_specs=out_specs, check_vma=False)
```

```python
import jax
import jax.numpy as jnp
from jax import lax
from jax.sharding import PartitionSpec as P
from jax.experimental import pallas as pl
from jax.experimental.pallas import tpu as pltpu

ITERS = 2


huber_edge = 1.5


def _band_mix_kernel(present_ref, mat_ref, rhs_ref, mask_ref, out_ref, acc_ref):
    acc_ref[...] = jnp.zeros(acc_ref.shape, jnp.float32)
    for band in range(mat_ref.shape[1]):

        @pl.when(present_ref[band] > 0)
        def _():
            masked = rhs_ref[0] * mask_ref[band : band + 1, :]
            acc_ref[...] += jnp.dot(mat_ref[0, band], masked, preferred_element_type=jnp.float32)

    out_ref[0] = acc_ref[...].astype(out_ref.dtype)


def band_mix(present, mats, rhs, mask, out_dtype, block=2048):
    count, bands, rows, inner = mats.shape
    columns = rhs.shape[2]
    return pl.pallas_call(
        _band_mix_kernel,
        grid_spec=pltpu.PrefetchScalarGridSpec(
            num_scalar_prefetch=1,
            grid=(count, columns // block),
            in_specs=[
                pl.BlockSpec((1, bands, rows, inner), lambda v, i, p: (v, 0, 0, 0)),
                pl.BlockSpec((1, inner, block), lambda v, i, p: (v, 0, i)),
                pl.BlockSpec((bands, block), lambda v, i, p: (0, i)),
            ],
            out_specs=pl.BlockSpec((1, rows, block), lambda v, i, p: (v, 0, i)),
            scratch_shapes=[pltpu.VMEM((rows, block), jnp.float32)],
        ),
        out_shape=jax.ShapeDtypeStruct((count, rows, columns), out_dtype),
    )(present, mats, rhs, mask)


def split_bf16(values):
    high = lax.reduce_precision(values, exponent_bits=8, mantissa_bits=7)
    low = values - high
    return high.astype(jnp.bfloat16), low.astype(jnp.bfloat16)


def total_over(values, axes):
    count = lax.axis_size(axes)
    spread = jnp.broadcast_to(values[None, :], (count, values.shape[0]))
    return jnp.sum(lax.all_to_all(spread, axes, 0, 0, tiled=True), axis=0)


def filter_adjoint(pieces, lon_tiled, lat_tiled):
    half_lon = jnp.einsum(
        "vaxj,vablxt->vbljt", lon_tiled, pieces, preferred_element_type=jnp.float32
    ).astype(jnp.bfloat16)
    return jnp.einsum("vbljt,vbtk->vljk", half_lon, lat_tiled, preferred_element_type=jnp.float32)


def filter_forward(planes, lon_tiled, lat_tiled):
    smooth_lon = jnp.einsum(
        "vaxj,vljk->vlaxk", lon_tiled, planes, preferred_element_type=jnp.float32
    ).astype(jnp.bfloat16)
    return jnp.einsum(
        "vlaxm,vbtm->vablxt", smooth_lon, lat_tiled, preferred_element_type=jnp.float32
    ).astype(jnp.bfloat16)


def shards(innovations, obs_column, obs_scale, band_of_lat, balance, lon_filter, lat_filter):
    axes = ("gx", "gy")
    lon_parts = lax.axis_size("gx")
    lat_parts = lax.axis_size("gy")
    devices = lon_parts * lat_parts
    var_count, levels, obs_count = innovations.shape
    lon_full = lon_filter.shape[1]
    lat_full = lat_filter.shape[1]
    lon_tile = lon_full // lon_parts
    lat_tile = lat_full // lat_parts
    columns = lon_tile * lat_tile
    per_dev = levels // devices
    rows = var_count * levels
    lon_tiled = lon_filter.reshape(var_count, lon_parts, lon_tile, lon_full)
    lat_tiled = lat_filter.reshape(var_count, lat_parts, lat_tile, lat_full)
    inv_scale = obs_scale[:, :, None]
    one_hot = (
        obs_column[:, None] == jnp.arange(columns, dtype=jnp.int32)[None, :]
    ).astype(jnp.bfloat16)
    bands = balance.shape[0]
    band_hot = (
        band_of_lat[None, :] == jnp.arange(bands, dtype=jnp.int32)[:, None]
    ).astype(jnp.bfloat16)
    band_present = jnp.max(band_hot, axis=1).astype(jnp.int32)
    band_mask = jnp.broadcast_to(band_hot[:, None, :], (bands, lon_tile, lat_tile)).reshape(bands, columns)
    balance_adj = jnp.transpose(balance, (1, 0, 3, 2))
    balance_fwd = jnp.transpose(balance, (1, 0, 2, 3))
    one_hot_pair = jnp.concatenate([one_hot, one_hot], axis=0)
    control = None
    increment = None
    inc_obs = None
    for iteration in range(ITERS):
        if inc_obs is None:
            scaled = -innovations * inv_scale
        else:
            scaled = (inc_obs - innovations) * inv_scale
        weighted = jnp.clip(scaled, -huber_edge, huber_edge) * inv_scale
        w_high, w_low = split_bf16(weighted.reshape(rows, obs_count))
        forcing = jnp.dot(
            jnp.concatenate([w_high, w_low], axis=1),
            one_hot_pair,
            preferred_element_type=jnp.float32,
        ).astype(jnp.bfloat16)
        forcing = forcing.reshape(var_count, levels, columns)
        grad_parts = []
        gradients = []
        returns = []
        balanced_all = band_mix(band_present, balance_adj, forcing, band_mask, jnp.bfloat16, block=columns)
        for var in range(var_count):
            balanced = balanced_all[var]
            pieces = lax.all_to_all(
                balanced.reshape(devices, 2, per_dev * columns // 2), axes, 0, 0, tiled=True
            )
            tiled = pieces.reshape(lon_parts, lat_parts, per_dev, lon_tile, lat_tile)
            half_lon = jnp.einsum(
                "axj,ablxt->bljt", lon_tiled[var], tiled, preferred_element_type=jnp.float32
            ).astype(jnp.bfloat16)
            adjoint = jnp.einsum("bljt,btk->ljk", half_lon, lat_tiled[var], preferred_element_type=jnp.float32)
            gradient = adjoint if control is None else control[var] + adjoint
            grad_parts.append(jnp.sum(gradient * gradient))
            gradients.append(gradient)
            smooth_lon = jnp.einsum(
                "axj,ljk->laxk", lon_tiled[var], gradient.astype(jnp.bfloat16), preferred_element_type=jnp.float32
            ).astype(jnp.bfloat16)
            smoothed = jnp.einsum(
                "laxm,btm->ablxt", smooth_lon, lat_tiled[var], preferred_element_type=jnp.float32
            ).astype(jnp.bfloat16)
            returned = lax.all_to_all(
                smoothed.reshape(devices, 2, per_dev * columns // 2), axes, 0, 0, tiled=True
            ).reshape(levels, columns)
            returns.append(returned)
        response = band_mix(band_present, balance_fwd, jnp.stack(returns), band_mask, jnp.float32, block=columns)
        r_high, r_low = split_bf16(response)
        at_obs = jnp.einsum(
            "vlc,jc->vlj", r_high, one_hot, preferred_element_type=jnp.float32
        ) + jnp.einsum("vlc,jc->vlj", r_low, one_hot, preferred_element_type=jnp.float32)
        gradient = jnp.stack(gradients)
        grad_local = sum(grad_parts)
        weight = huber_edge / jnp.maximum(jnp.abs(scaled), huber_edge)
        curve_local = jnp.sum(weight * (inv_scale * at_obs) ** 2)
        totals = total_over(jnp.stack([grad_local, curve_local]), axes)
        grad_norm = totals[0]
        curvature = totals[1]
        step_size = grad_norm / (grad_norm + curvature)
        if control is None:
            control = -(step_size * gradient)
            increment = -(step_size * response)
            inc_obs = -(step_size * at_obs)
        else:
            control = control - step_size * gradient
            increment = increment - step_size * response
            inc_obs = inc_obs - step_size * at_obs
    return (control, increment.reshape(var_count, levels, lon_tile, lat_tile))


def solution(mesh):
    in_specs = (P(None, None, ("gx", "gy")), P(("gx", "gy")), P(), P("gy"), P(), P(), P())
    out_specs = (P(None, ("gx", "gy"), None, None), P(None, None, "gx", "gy"))
    return jax.shard_map(shards, mesh=mesh, in_specs=in_specs, out_specs=out_specs, check_vma=False)
```

```python
import jax
import jax.numpy as jnp
from jax import lax
from jax.sharding import PartitionSpec as P
from jax.experimental import pallas as pl
from jax.experimental.pallas import tpu as pltpu

ITERS = 2


huber_edge = 1.5


def _band_mix_kernel(present_ref, mat_ref, rhs_ref, mask_ref, out_ref, acc_ref):
    acc_ref[...] = jnp.zeros(acc_ref.shape, jnp.float32)
    for band in range(mat_ref.shape[1]):

        @pl.when(present_ref[band] > 0)
        def _():
            masked = rhs_ref[...] * mask_ref[band : band + 1, :]
            acc_ref[...] += jnp.dot(mat_ref[0, band], masked, preferred_element_type=jnp.float32)

    out_ref[...] = acc_ref[...].astype(out_ref.dtype)


def band_mix(present, mats, rhs, mask, out_dtype):
    count, bands, rows, inner = mats.shape
    columns = mask.shape[1]
    return pl.pallas_call(
        _band_mix_kernel,
        grid_spec=pltpu.PrefetchScalarGridSpec(
            num_scalar_prefetch=1,
            grid=(count,),
            in_specs=[
                pl.BlockSpec((1, bands, rows, inner), lambda v, p: (v, 0, 0, 0)),
                pl.BlockSpec((inner, columns), lambda v, p: (0, v)),
                pl.BlockSpec((bands, columns), lambda v, p: (0, 0)),
            ],
            out_specs=pl.BlockSpec((rows, columns), lambda v, p: (0, v)),
            scratch_shapes=[pltpu.VMEM((rows, columns), jnp.float32)],
        ),
        out_shape=jax.ShapeDtypeStruct((rows, count * columns), out_dtype),
    )(present, mats, rhs, mask)


def split_bf16(values):
    high = lax.reduce_precision(values, exponent_bits=8, mantissa_bits=7)
    low = values - high
    return high.astype(jnp.bfloat16), low.astype(jnp.bfloat16)


def total_over(values, axes):
    count = lax.axis_size(axes)
    spread = jnp.broadcast_to(values[None, :], (count, values.shape[0]))
    return jnp.sum(lax.all_to_all(spread, axes, 0, 0, tiled=True), axis=0)


def filter_adjoint(pieces, lon_tiled, lat_tiled):
    half_lon = jnp.einsum(
        "vaxj,vablxt->vbljt", lon_tiled, pieces, preferred_element_type=jnp.float32
    ).astype(jnp.bfloat16)
    return jnp.einsum("vbljt,vbtk->vljk", half_lon, lat_tiled, preferred_element_type=jnp.float32)


def filter_forward(planes, lon_tiled, lat_tiled):
    smooth_lon = jnp.einsum(
        "vaxj,vljk->vlaxk", lon_tiled, planes, preferred_element_type=jnp.float32
    ).astype(jnp.bfloat16)
    return jnp.einsum(
        "vlaxm,vbtm->vablxt", smooth_lon, lat_tiled, preferred_element_type=jnp.float32
    ).astype(jnp.bfloat16)


def shards(innovations, obs_column, obs_scale, band_of_lat, balance, lon_filter, lat_filter):
    axes = ("gx", "gy")
    lon_parts = lax.axis_size("gx")
    lat_parts = lax.axis_size("gy")
    devices = lon_parts * lat_parts
    var_count, levels, obs_count = innovations.shape
    lon_full = lon_filter.shape[1]
    lat_full = lat_filter.shape[1]
    lon_tile = lon_full // lon_parts
    lat_tile = lat_full // lat_parts
    columns = lon_tile * lat_tile
    per_dev = levels // devices
    rows = var_count * levels
    lon_tiled = lon_filter.reshape(var_count, lon_parts, lon_tile, lon_full)
    lat_tiled = lat_filter.reshape(var_count, lat_parts, lat_tile, lat_full)
    inv_scale = obs_scale[:, :, None]
    one_hot = (
        obs_column[:, None] == jnp.arange(columns, dtype=jnp.int32)[None, :]
    ).astype(jnp.bfloat16)
    bands = balance.shape[0]
    band_hot = (
        band_of_lat[None, :] == jnp.arange(bands, dtype=jnp.int32)[:, None]
    ).astype(jnp.bfloat16)
    band_present = jnp.max(band_hot, axis=1).astype(jnp.int32)
    band_mask = jnp.broadcast_to(band_hot[:, None, :], (bands, lon_tile, lat_tile)).reshape(bands, columns)
    balance_adj = jnp.transpose(balance, (1, 0, 3, 2))
    balance_fwd = jnp.transpose(balance, (1, 0, 2, 3))
    one_hot_pair = jnp.concatenate([one_hot, one_hot], axis=0)
    control = None
    increment = None
    inc_obs = None
    for iteration in range(ITERS):
        if inc_obs is None:
            scaled = -innovations * inv_scale
        else:
            scaled = (inc_obs - innovations) * inv_scale
        weighted = jnp.clip(scaled, -huber_edge, huber_edge) * inv_scale
        w_high, w_low = split_bf16(weighted.reshape(rows, obs_count))
        forcing = jnp.dot(
            jnp.concatenate([w_high, w_low], axis=1),
            one_hot_pair,
            preferred_element_type=jnp.float32,
        ).astype(jnp.bfloat16)
        forcing = forcing.reshape(var_count, levels, columns)
        grad_parts = []
        gradients = []
        returns = []
        forcing_wide = jnp.concatenate([forcing[var] for var in range(var_count)], axis=1)
        balanced = band_mix(band_present, balance_adj, forcing_wide, band_mask, jnp.bfloat16)
        pieces = lax.all_to_all(
            balanced.reshape(devices, var_count, per_dev * columns), axes, 0, 0, tiled=True
        )
        for var in range(var_count):
            tiled = pieces[:, var].reshape(lon_parts, lat_parts, per_dev, lon_tile, lat_tile)
            half_lon = jnp.einsum(
                "axj,ablxt->bljt", lon_tiled[var], tiled, preferred_element_type=jnp.float32
            ).astype(jnp.bfloat16)
            adjoint = jnp.einsum("bljt,btk->ljk", half_lon, lat_tiled[var], preferred_element_type=jnp.float32)
            gradient = adjoint if control is None else control[var] + adjoint
            grad_parts.append(jnp.sum(gradient * gradient))
            gradients.append(gradient)
            smooth_lon = jnp.einsum(
                "axj,ljk->laxk", lon_tiled[var], gradient.astype(jnp.bfloat16), preferred_element_type=jnp.float32
            ).astype(jnp.bfloat16)
            smoothed = jnp.einsum(
                "laxm,btm->ablxt", smooth_lon, lat_tiled[var], preferred_element_type=jnp.float32
            ).astype(jnp.bfloat16)
            returns.append(smoothed.reshape(devices, per_dev * columns))
        returned = lax.all_to_all(jnp.stack(returns, axis=1), axes, 0, 0, tiled=True)
        response_wide = band_mix(
            band_present, balance_fwd, returned.reshape(levels, var_count * columns), band_mask, jnp.float32
        )
        response = response_wide
        r_high, r_low = split_bf16(response)
        at_obs = jnp.stack(
            [
                jnp.einsum(
                    "lc,jc->lj", r_high[:, var * columns : (var + 1) * columns], one_hot,
                    preferred_element_type=jnp.float32,
                )
                + jnp.einsum(
                    "lc,jc->lj", r_low[:, var * columns : (var + 1) * columns], one_hot,
                    preferred_element_type=jnp.float32,
                )
                for var in range(var_count)
            ]
        )
        gradient = jnp.stack(gradients)
        grad_local = sum(grad_parts)
        weight = huber_edge / jnp.maximum(jnp.abs(scaled), huber_edge)
        curve_local = jnp.sum(weight * (inv_scale * at_obs) ** 2)
        totals = total_over(jnp.stack([grad_local, curve_local]), axes)
        grad_norm = totals[0]
        curvature = totals[1]
        step_size = grad_norm / (grad_norm + curvature)
        if control is None:
            control = -(step_size * gradient)
            increment = -(step_size * response)
            inc_obs = -(step_size * at_obs)
        else:
            control = control - step_size * gradient
            increment = increment - step_size * response
            inc_obs = inc_obs - step_size * at_obs
    increment = jnp.transpose(increment.reshape(levels, var_count, lon_tile, lat_tile), (1, 0, 2, 3))
    return (control, increment)


def solution(mesh):
    in_specs = (P(None, None, ("gx", "gy")), P(("gx", "gy")), P(), P("gy"), P(), P(), P())
    out_specs = (P(None, ("gx", "gy"), None, None), P(None, None, "gx", "gy"))
    return jax.shard_map(shards, mesh=mesh, in_specs=in_specs, out_specs=out_specs, check_vma=False)
```

```python
import jax
import jax.numpy as jnp
from jax import lax
from jax.sharding import PartitionSpec as P
from jax.experimental import pallas as pl
from jax.experimental.pallas import tpu as pltpu

ITERS = 2


huber_edge = 1.5


def _band_mix_kernel(present_ref, mat_ref, rhs_ref, mask_ref, out_ref, acc_ref):
    acc_ref[...] = jnp.zeros(acc_ref.shape, jnp.float32)
    for band in range(mat_ref.shape[1]):

        @pl.when(present_ref[band] > 0)
        def _():
            masked = rhs_ref[0] * mask_ref[band : band + 1, :]
            acc_ref[...] += jnp.dot(mat_ref[0, band], masked, preferred_element_type=jnp.float32)

    out_ref[0] = acc_ref[...].astype(out_ref.dtype)


def band_mix(present, mats, rhs, mask, out_dtype, block=2048):
    count, bands, rows, inner = mats.shape
    columns = rhs.shape[2]
    return pl.pallas_call(
        _band_mix_kernel,
        grid_spec=pltpu.PrefetchScalarGridSpec(
            num_scalar_prefetch=1,
            grid=(count, columns // block),
            in_specs=[
                pl.BlockSpec((1, bands, rows, inner), lambda v, i, p: (v, 0, 0, 0)),
                pl.BlockSpec((1, inner, block), lambda v, i, p: (v, 0, i)),
                pl.BlockSpec((bands, block), lambda v, i, p: (0, i)),
            ],
            out_specs=pl.BlockSpec((1, rows, block), lambda v, i, p: (v, 0, i)),
            scratch_shapes=[pltpu.VMEM((rows, block), jnp.float32)],
        ),
        out_shape=jax.ShapeDtypeStruct((count, rows, columns), out_dtype),
    )(present, mats, rhs, mask)


def split_bf16(values):
    high = lax.reduce_precision(values, exponent_bits=8, mantissa_bits=7)
    low = values - high
    return high.astype(jnp.bfloat16), low.astype(jnp.bfloat16)


def total_over(values, axes):
    count = lax.axis_size(axes)
    spread = jnp.broadcast_to(values[None, :], (count, values.shape[0]))
    return jnp.sum(lax.all_to_all(spread, axes, 0, 0, tiled=True), axis=0)


def filter_adjoint(pieces, lon_tiled, lat_tiled):
    half_lon = jnp.einsum(
        "vaxj,vablxt->vbljt", lon_tiled, pieces, preferred_element_type=jnp.float32
    ).astype(jnp.bfloat16)
    return jnp.einsum("vbljt,vbtk->vljk", half_lon, lat_tiled, preferred_element_type=jnp.float32)


def filter_forward(planes, lon_tiled, lat_tiled):
    smooth_lon = jnp.einsum(
        "vaxj,vljk->vlaxk", lon_tiled, planes, preferred_element_type=jnp.float32
    ).astype(jnp.bfloat16)
    return jnp.einsum(
        "vlaxm,vbtm->vablxt", smooth_lon, lat_tiled, preferred_element_type=jnp.float32
    ).astype(jnp.bfloat16)


def shards(innovations, obs_column, obs_scale, band_of_lat, balance, lon_filter, lat_filter):
    axes = ("gx", "gy")
    lon_parts = lax.axis_size("gx")
    lat_parts = lax.axis_size("gy")
    devices = lon_parts * lat_parts
    var_count, levels, obs_count = innovations.shape
    lon_full = lon_filter.shape[1]
    lat_full = lat_filter.shape[1]
    lon_tile = lon_full // lon_parts
    lat_tile = lat_full // lat_parts
    columns = lon_tile * lat_tile
    per_dev = levels // devices
    rows = var_count * levels
    lon_tiled = lon_filter.reshape(var_count, lon_parts, lon_tile, lon_full)
    lat_tiled = lat_filter.reshape(var_count, lat_parts, lat_tile, lat_full)
    inv_scale = obs_scale[:, :, None]
    one_hot = (
        obs_column[:, None] == jnp.arange(columns, dtype=jnp.int32)[None, :]
    ).astype(jnp.bfloat16)
    bands = balance.shape[0]
    band_hot = (
        band_of_lat[None, :] == jnp.arange(bands, dtype=jnp.int32)[:, None]
    ).astype(jnp.bfloat16)
    band_present = jnp.max(band_hot, axis=1).astype(jnp.int32)
    band_mask = jnp.broadcast_to(band_hot[:, None, :], (bands, lon_tile, lat_tile)).reshape(bands, columns)
    balance_adj = jnp.transpose(balance, (1, 0, 3, 2))
    balance_fwd = jnp.transpose(balance, (1, 0, 2, 3))
    one_hot_pair = jnp.concatenate([one_hot, one_hot], axis=0)
    control = None
    increment = None
    inc_obs = None
    for iteration in range(ITERS):
        if inc_obs is None:
            scaled = -innovations * inv_scale
        else:
            scaled = (inc_obs - innovations) * inv_scale
        weighted = jnp.clip(scaled, -huber_edge, huber_edge) * inv_scale
        w_high, w_low = split_bf16(weighted.reshape(rows, obs_count))
        forcing = jnp.dot(
            jnp.concatenate([w_high, w_low], axis=1),
            one_hot_pair,
            preferred_element_type=jnp.float32,
        ).astype(jnp.bfloat16)
        forcing = forcing.reshape(var_count, levels, columns)
        grad_parts = []
        gradients = []
        returns = []
        obs_parts = []
        balanced_all = band_mix(band_present, balance_adj, forcing, band_mask, jnp.bfloat16, block=columns)
        for var in range(var_count):
            balanced = balanced_all[var]
            pieces = lax.all_to_all(
                balanced.reshape(devices, 2, per_dev * columns // 2), axes, 0, 0, tiled=True
            )
            tiled = pieces.reshape(lon_parts, lat_parts, per_dev, lon_tile, lat_tile)
            half_lon = jnp.einsum(
                "axj,ablxt->bljt", lon_tiled[var], tiled, preferred_element_type=jnp.float32
            ).astype(jnp.bfloat16)
            adjoint = jnp.einsum("bljt,btk->ljk", half_lon, lat_tiled[var], preferred_element_type=jnp.float32)
            gradient = adjoint if control is None else control[var] + adjoint
            grad_parts.append(jnp.sum(gradient * gradient))
            gradients.append(gradient)
            smooth_lon = jnp.einsum(
                "axj,ljk->laxk", lon_tiled[var], gradient.astype(jnp.bfloat16), preferred_element_type=jnp.float32
            ).astype(jnp.bfloat16)
            smoothed = jnp.einsum(
                "laxm,btm->ablxt", smooth_lon, lat_tiled[var], preferred_element_type=jnp.float32
            ).astype(jnp.bfloat16)
            returned = lax.all_to_all(
                smoothed.reshape(devices, 2, per_dev * columns // 2), axes, 0, 0, tiled=True
            ).reshape(levels, columns)
            response_var = band_mix(
                band_present, balance_fwd[var : var + 1], returned[None], band_mask, jnp.float32, block=columns
            )[0]
            returns.append(response_var)
            r_high, r_low = split_bf16(response_var)
            obs_parts.append(
                jnp.einsum("lc,jc->lj", r_high, one_hot, preferred_element_type=jnp.float32)
                + jnp.einsum("lc,jc->lj", r_low, one_hot, preferred_element_type=jnp.float32)
            )
        response = jnp.stack(returns)
        at_obs = jnp.stack(obs_parts)
        gradient = jnp.stack(gradients)
        grad_local = sum(grad_parts)
        weight = huber_edge / jnp.maximum(jnp.abs(scaled), huber_edge)
        curve_local = jnp.sum(weight * (inv_scale * at_obs) ** 2)
        totals = total_over(jnp.stack([grad_local, curve_local]), axes)
        grad_norm = totals[0]
        curvature = totals[1]
        step_size = grad_norm / (grad_norm + curvature)
        if control is None:
            control = -(step_size * gradient)
            increment = -(step_size * response)
            inc_obs = -(step_size * at_obs)
        else:
            control = control - step_size * gradient
            increment = increment - step_size * response
            inc_obs = inc_obs - step_size * at_obs
    return (control, increment.reshape(var_count, levels, lon_tile, lat_tile))


def solution(mesh):
    in_specs = (P(None, None, ("gx", "gy")), P(("gx", "gy")), P(), P("gy"), P(), P(), P())
    out_specs = (P(None, ("gx", "gy"), None, None), P(None, None, "gx", "gy"))
    return jax.shard_map(shards, mesh=mesh, in_specs=in_specs, out_specs=out_specs, check_vma=False)
```

```python
import jax
import jax.numpy as jnp
from jax import lax
from jax.sharding import PartitionSpec as P
from jax.experimental import pallas as pl
from jax.experimental.pallas import tpu as pltpu

ITERS = 2


huber_edge = 1.5


def _band_mix_kernel(present_ref, mat_ref, rhs_ref, mask_ref, out_ref, acc_ref):
    acc_ref[...] = jnp.zeros(acc_ref.shape, jnp.float32)
    for band in range(mat_ref.shape[1]):

        @pl.when(present_ref[band] > 0)
        def _():
            masked = rhs_ref[0] * mask_ref[band : band + 1, :]
            acc_ref[...] += jnp.dot(mat_ref[0, band], masked, preferred_element_type=jnp.float32)

    out_ref[0] = acc_ref[...].astype(out_ref.dtype)


def band_mix(present, mats, rhs, mask, out_dtype, block=2048):
    count, bands, rows, inner = mats.shape
    columns = rhs.shape[2]
    return pl.pallas_call(
        _band_mix_kernel,
        grid_spec=pltpu.PrefetchScalarGridSpec(
            num_scalar_prefetch=1,
            grid=(count, columns // block),
            in_specs=[
                pl.BlockSpec((1, bands, rows, inner), lambda v, i, p: (v, 0, 0, 0)),
                pl.BlockSpec((1, inner, block), lambda v, i, p: (v, 0, i)),
                pl.BlockSpec((bands, block), lambda v, i, p: (0, i)),
            ],
            out_specs=pl.BlockSpec((1, rows, block), lambda v, i, p: (v, 0, i)),
            scratch_shapes=[pltpu.VMEM((rows, block), jnp.float32)],
        ),
        out_shape=jax.ShapeDtypeStruct((count, rows, columns), out_dtype),
    )(present, mats, rhs, mask)


def split_bf16(values):
    high = lax.reduce_precision(values, exponent_bits=8, mantissa_bits=7)
    low = values - high
    return high.astype(jnp.bfloat16), low.astype(jnp.bfloat16)


def total_over(values, axes):
    count = lax.axis_size(axes)
    spread = jnp.broadcast_to(values[None, :], (count, values.shape[0]))
    return jnp.sum(lax.all_to_all(spread, axes, 0, 0, tiled=True), axis=0)


def filter_adjoint(pieces, lon_tiled, lat_tiled):
    half_lon = jnp.einsum(
        "vaxj,vablxt->vbljt", lon_tiled, pieces, preferred_element_type=jnp.float32
    ).astype(jnp.bfloat16)
    return jnp.einsum("vbljt,vbtk->vljk", half_lon, lat_tiled, preferred_element_type=jnp.float32)


def filter_forward(planes, lon_tiled, lat_tiled):
    smooth_lon = jnp.einsum(
        "vaxj,vljk->vlaxk", lon_tiled, planes, preferred_element_type=jnp.float32
    ).astype(jnp.bfloat16)
    return jnp.einsum(
        "vlaxm,vbtm->vablxt", smooth_lon, lat_tiled, preferred_element_type=jnp.float32
    ).astype(jnp.bfloat16)


def shards(innovations, obs_column, obs_scale, band_of_lat, balance, lon_filter, lat_filter):
    axes = ("gx", "gy")
    lon_parts = lax.axis_size("gx")
    lat_parts = lax.axis_size("gy")
    devices = lon_parts * lat_parts
    var_count, levels, obs_count = innovations.shape
    lon_full = lon_filter.shape[1]
    lat_full = lat_filter.shape[1]
    lon_tile = lon_full // lon_parts
    lat_tile = lat_full // lat_parts
    columns = lon_tile * lat_tile
    per_dev = levels // devices
    rows = var_count * levels
    lon_tiled = lon_filter.reshape(var_count, lon_parts, lon_tile, lon_full)
    lat_tiled = lat_filter.reshape(var_count, lat_parts, lat_tile, lat_full)
    inv_scale = obs_scale[:, :, None]
    one_hot = (
        obs_column[:, None] == jnp.arange(columns, dtype=jnp.int32)[None, :]
    ).astype(jnp.bfloat16)
    bands = balance.shape[0]
    band_hot = (
        band_of_lat[None, :] == jnp.arange(bands, dtype=jnp.int32)[:, None]
    ).astype(jnp.bfloat16)
    band_present = jnp.max(band_hot, axis=1).astype(jnp.int32)
    band_mask = jnp.broadcast_to(band_hot[:, None, :], (bands, lon_tile, lat_tile)).reshape(bands, columns)
    balance_adj = jnp.transpose(balance, (1, 0, 3, 2))
    balance_fwd = jnp.transpose(balance, (1, 0, 2, 3))
    one_hot_pair = jnp.concatenate([one_hot, one_hot], axis=0)
    control = None
    increment = None
    inc_obs = None
    for iteration in range(ITERS):
        if inc_obs is None:
            scaled = -innovations * inv_scale
        else:
            scaled = (inc_obs - innovations) * inv_scale
        weighted = jnp.clip(scaled, -huber_edge, huber_edge) * inv_scale
        w_high, w_low = split_bf16(weighted.reshape(rows, obs_count))
        forcing = jnp.dot(
            jnp.concatenate([w_high, w_low], axis=1),
            one_hot_pair,
            preferred_element_type=jnp.float32,
        ).astype(jnp.bfloat16)
        forcing = forcing.reshape(var_count, levels, columns)
        grad_parts = []
        gradients = []
        returns = []
        obs_parts = []
        for var in range(var_count):
            balanced = band_mix(
                band_present, balance_adj[var : var + 1], forcing[var][None], band_mask, jnp.bfloat16, block=columns
            )[0]
            pieces = lax.all_to_all(
                balanced.reshape(devices, 2, per_dev * columns // 2), axes, 0, 0, tiled=True
            )
            tiled = pieces.reshape(lon_parts, lat_parts, per_dev, lon_tile, lat_tile)
            half_lon = jnp.einsum(
                "axj,ablxt->bljt", lon_tiled[var], tiled, preferred_element_type=jnp.float32
            ).astype(jnp.bfloat16)
            adjoint = jnp.einsum("bljt,btk->ljk", half_lon, lat_tiled[var], preferred_element_type=jnp.float32)
            gradient = adjoint if control is None else control[var] + adjoint
            grad_parts.append(jnp.sum(gradient * gradient))
            gradients.append(gradient)
            smooth_lon = jnp.einsum(
                "axj,ljk->laxk", lon_tiled[var], gradient.astype(jnp.bfloat16), preferred_element_type=jnp.float32
            ).astype(jnp.bfloat16)
            smoothed = jnp.einsum(
                "laxm,btm->ablxt", smooth_lon, lat_tiled[var], preferred_element_type=jnp.float32
            ).astype(jnp.bfloat16)
            returned = lax.all_to_all(
                smoothed.reshape(devices, 2, per_dev * columns // 2), axes, 0, 0, tiled=True
            ).reshape(levels, columns)
            response_var = band_mix(
                band_present, balance_fwd[var : var + 1], returned[None], band_mask, jnp.float32, block=columns
            )[0]
            returns.append(response_var)
            r_high, r_low = split_bf16(response_var)
            obs_parts.append(
                jnp.einsum("lc,jc->lj", r_high, one_hot, preferred_element_type=jnp.float32)
                + jnp.einsum("lc,jc->lj", r_low, one_hot, preferred_element_type=jnp.float32)
            )
        response = jnp.stack(returns)
        at_obs = jnp.stack(obs_parts)
        gradient = jnp.stack(gradients)
        grad_local = sum(grad_parts)
        weight = huber_edge / jnp.maximum(jnp.abs(scaled), huber_edge)
        curve_local = jnp.sum(weight * (inv_scale * at_obs) ** 2)
        totals = total_over(jnp.stack([grad_local, curve_local]), axes)
        grad_norm = totals[0]
        curvature = totals[1]
        step_size = grad_norm / (grad_norm + curvature)
        if control is None:
            control = -(step_size * gradient)
            increment = -(step_size * response)
            inc_obs = -(step_size * at_obs)
        else:
            control = control - step_size * gradient
            increment = increment - step_size * response
            inc_obs = inc_obs - step_size * at_obs
    return (control, increment.reshape(var_count, levels, lon_tile, lat_tile))


def solution(mesh):
    in_specs = (P(None, None, ("gx", "gy")), P(("gx", "gy")), P(), P("gy"), P(), P(), P())
    out_specs = (P(None, ("gx", "gy"), None, None), P(None, None, "gx", "gy"))
    return jax.shard_map(shards, mesh=mesh, in_specs=in_specs, out_specs=out_specs, check_vma=False)
```

```python
import jax
import jax.numpy as jnp
from jax import lax
from jax.sharding import PartitionSpec as P
from jax.experimental import pallas as pl
from jax.experimental.pallas import tpu as pltpu

ITERS = 2


huber_edge = 1.5


def _band_mix_kernel(present_ref, mat_ref, rhs_ref, mask_ref, out_ref, acc_ref):
    acc_ref[...] = jnp.zeros(acc_ref.shape, jnp.float32)
    for band in range(mat_ref.shape[1]):

        @pl.when(present_ref[band] > 0)
        def _():
            masked = rhs_ref[0] * mask_ref[band : band + 1, :]
            acc_ref[...] += jnp.dot(mat_ref[0, band], masked, preferred_element_type=jnp.float32)

    out_ref[0] = acc_ref[...].astype(out_ref.dtype)


def band_mix(present, mats, rhs, mask, out_dtype, block=2048):
    count, bands, rows, inner = mats.shape
    columns = rhs.shape[2]
    return pl.pallas_call(
        _band_mix_kernel,
        grid_spec=pltpu.PrefetchScalarGridSpec(
            num_scalar_prefetch=1,
            grid=(count, columns // block),
            in_specs=[
                pl.BlockSpec((1, bands, rows, inner), lambda v, i, p: (v, 0, 0, 0)),
                pl.BlockSpec((1, inner, block), lambda v, i, p: (v, 0, i)),
                pl.BlockSpec((bands, block), lambda v, i, p: (0, i)),
            ],
            out_specs=pl.BlockSpec((1, rows, block), lambda v, i, p: (v, 0, i)),
            scratch_shapes=[pltpu.VMEM((rows, block), jnp.float32)],
        ),
        out_shape=jax.ShapeDtypeStruct((count, rows, columns), out_dtype),
    )(present, mats, rhs, mask)


def split_bf16(values):
    high = lax.reduce_precision(values, exponent_bits=8, mantissa_bits=7)
    low = values - high
    return high.astype(jnp.bfloat16), low.astype(jnp.bfloat16)


def total_over(values, axes):
    count = lax.axis_size(axes)
    spread = jnp.broadcast_to(values[None, :], (count, values.shape[0]))
    return jnp.sum(lax.all_to_all(spread, axes, 0, 0, tiled=True), axis=0)


def filter_adjoint(pieces, lon_tiled, lat_tiled):
    half_lon = jnp.einsum(
        "vaxj,vablxt->vbljt", lon_tiled, pieces, preferred_element_type=jnp.float32
    ).astype(jnp.bfloat16)
    return jnp.einsum("vbljt,vbtk->vljk", half_lon, lat_tiled, preferred_element_type=jnp.float32)


def filter_forward(planes, lon_tiled, lat_tiled):
    smooth_lon = jnp.einsum(
        "vaxj,vljk->vlaxk", lon_tiled, planes, preferred_element_type=jnp.float32
    ).astype(jnp.bfloat16)
    return jnp.einsum(
        "vlaxm,vbtm->vablxt", smooth_lon, lat_tiled, preferred_element_type=jnp.float32
    ).astype(jnp.bfloat16)


def shards(innovations, obs_column, obs_scale, band_of_lat, balance, lon_filter, lat_filter):
    axes = ("gx", "gy")
    lon_parts = lax.axis_size("gx")
    lat_parts = lax.axis_size("gy")
    devices = lon_parts * lat_parts
    var_count, levels, obs_count = innovations.shape
    lon_full = lon_filter.shape[1]
    lat_full = lat_filter.shape[1]
    lon_tile = lon_full // lon_parts
    lat_tile = lat_full // lat_parts
    columns = lon_tile * lat_tile
    per_dev = levels // devices
    rows = var_count * levels
    lon_tiled = lon_filter.reshape(var_count, lon_parts, lon_tile, lon_full)
    lat_tiled = lat_filter.reshape(var_count, lat_parts, lat_tile, lat_full)
    inv_scale = obs_scale[:, :, None]
    one_hot = (
        obs_column[:, None] == jnp.arange(columns, dtype=jnp.int32)[None, :]
    ).astype(jnp.bfloat16)
    bands = balance.shape[0]
    band_hot = (
        band_of_lat[None, :] == jnp.arange(bands, dtype=jnp.int32)[:, None]
    ).astype(jnp.bfloat16)
    band_present = jnp.max(band_hot, axis=1).astype(jnp.int32)
    band_mask = jnp.broadcast_to(band_hot[:, None, :], (bands, lon_tile, lat_tile)).reshape(bands, columns)
    balance_adj = jnp.transpose(balance, (1, 0, 3, 2))
    balance_fwd = jnp.transpose(balance, (1, 0, 2, 3))
    one_hot_pair = jnp.concatenate([one_hot, one_hot], axis=0)
    def iteration_step(_, carry):
        control, increment, inc_obs = carry
        scaled = (inc_obs - innovations) * inv_scale
        weighted = jnp.clip(scaled, -huber_edge, huber_edge) * inv_scale
        w_high, w_low = split_bf16(weighted.reshape(rows, obs_count))
        forcing = jnp.dot(
            jnp.concatenate([w_high, w_low], axis=1),
            one_hot_pair,
            preferred_element_type=jnp.float32,
        ).astype(jnp.bfloat16)
        forcing = forcing.reshape(var_count, levels, columns)
        grad_parts = []
        gradients = []
        returns = []
        obs_parts = []
        balanced_all = band_mix(band_present, balance_adj, forcing, band_mask, jnp.bfloat16, block=columns)
        for var in range(var_count):
            balanced = balanced_all[var]
            pieces = lax.all_to_all(
                balanced.reshape(devices, 2, per_dev * columns // 2), axes, 0, 0, tiled=True
            )
            tiled = pieces.reshape(lon_parts, lat_parts, per_dev, lon_tile, lat_tile)
            half_lon = jnp.einsum(
                "axj,ablxt->bljt", lon_tiled[var], tiled, preferred_element_type=jnp.float32
            ).astype(jnp.bfloat16)
            adjoint = jnp.einsum("bljt,btk->ljk", half_lon, lat_tiled[var], preferred_element_type=jnp.float32)
            gradient = control[var] + adjoint
            grad_parts.append(jnp.sum(gradient * gradient))
            gradients.append(gradient)
            smooth_lon = jnp.einsum(
                "axj,ljk->laxk", lon_tiled[var], gradient.astype(jnp.bfloat16), preferred_element_type=jnp.float32
            ).astype(jnp.bfloat16)
            smoothed = jnp.einsum(
                "laxm,btm->ablxt", smooth_lon, lat_tiled[var], preferred_element_type=jnp.float32
            ).astype(jnp.bfloat16)
            returned = lax.all_to_all(
                smoothed.reshape(devices, 2, per_dev * columns // 2), axes, 0, 0, tiled=True
            ).reshape(levels, columns)
            response_var = band_mix(
                band_present, balance_fwd[var : var + 1], returned[None], band_mask, jnp.float32, block=columns
            )[0]
            returns.append(response_var)
            r_high, r_low = split_bf16(response_var)
            obs_parts.append(
                jnp.einsum("lc,jc->lj", r_high, one_hot, preferred_element_type=jnp.float32)
                + jnp.einsum("lc,jc->lj", r_low, one_hot, preferred_element_type=jnp.float32)
            )
        response = jnp.stack(returns)
        at_obs = jnp.stack(obs_parts)
        gradient = jnp.stack(gradients)
        grad_local = sum(grad_parts)
        weight = huber_edge / jnp.maximum(jnp.abs(scaled), huber_edge)
        curve_local = jnp.sum(weight * (inv_scale * at_obs) ** 2)
        totals = total_over(jnp.stack([grad_local, curve_local]), axes)
        grad_norm = totals[0]
        curvature = totals[1]
        step_size = grad_norm / (grad_norm + curvature)
        control = control - step_size * gradient
        increment = increment - step_size * response
        inc_obs = inc_obs - step_size * at_obs
        return control, increment, inc_obs

    start = (
        jnp.zeros((var_count, per_dev, lon_full, lat_full), jnp.float32),
        jnp.zeros((var_count, levels, columns), jnp.float32),
        jnp.zeros((var_count, levels, obs_count), jnp.float32),
    )
    control, increment, inc_obs = lax.fori_loop(0, ITERS, iteration_step, start)
    return (control, increment.reshape(var_count, levels, lon_tile, lat_tile))


def solution(mesh):
    in_specs = (P(None, None, ("gx", "gy")), P(("gx", "gy")), P(), P("gy"), P(), P(), P())
    out_specs = (P(None, ("gx", "gy"), None, None), P(None, None, "gx", "gy"))
    return jax.shard_map(shards, mesh=mesh, in_specs=in_specs, out_specs=out_specs, check_vma=False)
```

```python
import functools

import jax
import jax.numpy as jnp
from jax import lax
from jax.sharding import PartitionSpec as P
from jax.experimental import pallas as pl
from jax.experimental.pallas import tpu as pltpu

ITERS = 2


huber_edge = 1.5


def _band_mix_kernel(present_ref, mat_ref, rhs_ref, mask_ref, out_ref, acc_ref, *, transpose):
    acc_ref[...] = jnp.zeros(acc_ref.shape, jnp.float32)
    contract = 0 if transpose else 1
    for band in range(mat_ref.shape[0]):

        @pl.when(present_ref[band] > 0)
        def _():
            masked = rhs_ref[0] * mask_ref[band : band + 1, :]
            acc_ref[...] += lax.dot_general(
                mat_ref[band, 0], masked, (((contract,), (0,)), ((), ())), preferred_element_type=jnp.float32
            )

    out_ref[0] = acc_ref[...].astype(out_ref.dtype)


def band_mix(present, balance, first, rhs, mask, out_dtype, transpose):
    bands = balance.shape[0]
    count, inner, columns = rhs.shape
    rows = balance.shape[3] if transpose else balance.shape[2]
    return pl.pallas_call(
        functools.partial(_band_mix_kernel, transpose=transpose),
        grid_spec=pltpu.PrefetchScalarGridSpec(
            num_scalar_prefetch=1,
            grid=(count,),
            in_specs=[
                pl.BlockSpec((bands, 1) + balance.shape[2:], lambda v, p: (0, first + v, 0, 0)),
                pl.BlockSpec((1, inner, columns), lambda v, p: (v, 0, 0)),
                pl.BlockSpec((bands, columns), lambda v, p: (0, 0)),
            ],
            out_specs=pl.BlockSpec((1, rows, columns), lambda v, p: (v, 0, 0)),
            scratch_shapes=[pltpu.VMEM((rows, columns), jnp.float32)],
        ),
        out_shape=jax.ShapeDtypeStruct((count, rows, columns), out_dtype),
    )(present, balance, rhs, mask)


def split_bf16(values):
    high = lax.reduce_precision(values, exponent_bits=8, mantissa_bits=7)
    low = values - high
    return high.astype(jnp.bfloat16), low.astype(jnp.bfloat16)


def total_over(values, axes):
    count = lax.axis_size(axes)
    spread = jnp.broadcast_to(values[None, :], (count, values.shape[0]))
    return jnp.sum(lax.all_to_all(spread, axes, 0, 0, tiled=True), axis=0)


def filter_adjoint(pieces, lon_tiled, lat_tiled):
    half_lon = jnp.einsum(
        "vaxj,vablxt->vbljt", lon_tiled, pieces, preferred_element_type=jnp.float32
    ).astype(jnp.bfloat16)
    return jnp.einsum("vbljt,vbtk->vljk", half_lon, lat_tiled, preferred_element_type=jnp.float32)


def filter_forward(planes, lon_tiled, lat_tiled):
    smooth_lon = jnp.einsum(
        "vaxj,vljk->vlaxk", lon_tiled, planes, preferred_element_type=jnp.float32
    ).astype(jnp.bfloat16)
    return jnp.einsum(
        "vlaxm,vbtm->vablxt", smooth_lon, lat_tiled, preferred_element_type=jnp.float32
    ).astype(jnp.bfloat16)


def shards(innovations, obs_column, obs_scale, band_of_lat, balance, lon_filter, lat_filter):
    axes = ("gx", "gy")
    lon_parts = lax.axis_size("gx")
    lat_parts = lax.axis_size("gy")
    devices = lon_parts * lat_parts
    var_count, levels, obs_count = innovations.shape
    lon_full = lon_filter.shape[1]
    lat_full = lat_filter.shape[1]
    lon_tile = lon_full // lon_parts
    lat_tile = lat_full // lat_parts
    columns = lon_tile * lat_tile
    per_dev = levels // devices
    rows = var_count * levels
    lon_tiled = lon_filter.reshape(var_count, lon_parts, lon_tile, lon_full)
    lat_tiled = lat_filter.reshape(var_count, lat_parts, lat_tile, lat_full)
    inv_scale = obs_scale[:, :, None]
    one_hot = (
        obs_column[:, None] == jnp.arange(columns, dtype=jnp.int32)[None, :]
    ).astype(jnp.bfloat16)
    bands = balance.shape[0]
    band_hot = (
        band_of_lat[None, :] == jnp.arange(bands, dtype=jnp.int32)[:, None]
    ).astype(jnp.bfloat16)
    band_present = jnp.max(band_hot, axis=1).astype(jnp.int32)
    band_mask = jnp.broadcast_to(band_hot[:, None, :], (bands, lon_tile, lat_tile)).reshape(bands, columns)
    one_hot_pair = jnp.concatenate([one_hot, one_hot], axis=0)
    control = None
    increment = None
    inc_obs = None
    for iteration in range(ITERS):
        if inc_obs is None:
            scaled = -innovations * inv_scale
        else:
            scaled = (inc_obs - innovations) * inv_scale
        weighted = jnp.clip(scaled, -huber_edge, huber_edge) * inv_scale
        w_high, w_low = split_bf16(weighted.reshape(rows, obs_count))
        forcing = jnp.dot(
            jnp.concatenate([w_high, w_low], axis=1),
            one_hot_pair,
            preferred_element_type=jnp.float32,
        ).astype(jnp.bfloat16)
        forcing = forcing.reshape(var_count, levels, columns)
        grad_parts = []
        gradients = []
        returns = []
        obs_parts = []
        balanced_all = band_mix(band_present, balance, 0, forcing, band_mask, jnp.bfloat16, True)
        for var in range(var_count):
            balanced = balanced_all[var]
            pieces = lax.all_to_all(
                balanced.reshape(devices, 2, per_dev * columns // 2), axes, 0, 0, tiled=True
            )
            tiled = pieces.reshape(lon_parts, lat_parts, per_dev, lon_tile, lat_tile)
            half_lon = jnp.einsum(
                "axj,ablxt->bljt", lon_tiled[var], tiled, preferred_element_type=jnp.float32
            ).astype(jnp.bfloat16)
            adjoint = jnp.einsum("bljt,btk->ljk", half_lon, lat_tiled[var], preferred_element_type=jnp.float32)
            gradient = adjoint if control is None else control[var] + adjoint
            grad_parts.append(jnp.sum(gradient * gradient))
            gradients.append(gradient)
            smooth_lon = jnp.einsum(
                "axj,ljk->laxk", lon_tiled[var], gradient.astype(jnp.bfloat16), preferred_element_type=jnp.float32
            ).astype(jnp.bfloat16)
            smoothed = jnp.einsum(
                "laxm,btm->ablxt", smooth_lon, lat_tiled[var], preferred_element_type=jnp.float32
            ).astype(jnp.bfloat16)
            returned = lax.all_to_all(
                smoothed.reshape(devices, 2, per_dev * columns // 2), axes, 0, 0, tiled=True
            ).reshape(levels, columns)
            response_var = band_mix(
                band_present, balance, var, returned[None], band_mask, jnp.float32, False
            )[0]
            returns.append(response_var)
            r_high, r_low = split_bf16(response_var)
            obs_parts.append(
                jnp.einsum("lc,jc->lj", r_high, one_hot, preferred_element_type=jnp.float32)
                + jnp.einsum("lc,jc->lj", r_low, one_hot, preferred_element_type=jnp.float32)
            )
        response = jnp.stack(returns)
        at_obs = jnp.stack(obs_parts)
        gradient = jnp.stack(gradients)
        grad_local = sum(grad_parts)
        weight = huber_edge / jnp.maximum(jnp.abs(scaled), huber_edge)
        curve_local = jnp.sum(weight * (inv_scale * at_obs) ** 2)
        totals = total_over(jnp.stack([grad_local, curve_local]), axes)
        grad_norm = totals[0]
        curvature = totals[1]
        step_size = grad_norm / (grad_norm + curvature)
        if control is None:
            control = -(step_size * gradient)
            increment = -(step_size * response)
            inc_obs = -(step_size * at_obs)
        else:
            control = control - step_size * gradient
            increment = increment - step_size * response
            inc_obs = inc_obs - step_size * at_obs
    return (control, increment.reshape(var_count, levels, lon_tile, lat_tile))


def solution(mesh):
    in_specs = (P(None, None, ("gx", "gy")), P(("gx", "gy")), P(), P("gy"), P(), P(), P())
    out_specs = (P(None, ("gx", "gy"), None, None), P(None, None, "gx", "gy"))
    return jax.shard_map(shards, mesh=mesh, in_specs=in_specs, out_specs=out_specs, check_vma=False)
```

```python
import jax
import jax.numpy as jnp
from jax import lax
from jax.sharding import PartitionSpec as P
from jax.experimental import pallas as pl
from jax.experimental.pallas import tpu as pltpu

ITERS = 2


huber_edge = 1.5


def _band_mix_kernel(present_ref, mat_ref, rhs_ref, mask_ref, out_ref, acc_ref):
    acc_ref[...] = jnp.zeros(acc_ref.shape, jnp.float32)
    for band in range(mat_ref.shape[1]):

        @pl.when(present_ref[band] > 0)
        def _():
            masked = rhs_ref[0] * mask_ref[band : band + 1, :]
            acc_ref[...] += jnp.dot(mat_ref[0, band], masked, preferred_element_type=jnp.float32)

    out_ref[0] = acc_ref[...].astype(out_ref.dtype)


def band_mix(present, mats, rhs, mask, out_dtype, block=2048):
    count, bands, rows, inner = mats.shape
    columns = rhs.shape[2]
    return pl.pallas_call(
        _band_mix_kernel,
        grid_spec=pltpu.PrefetchScalarGridSpec(
            num_scalar_prefetch=1,
            grid=(count, columns // block),
            in_specs=[
                pl.BlockSpec((1, bands, rows, inner), lambda v, i, p: (v, 0, 0, 0)),
                pl.BlockSpec((1, inner, block), lambda v, i, p: (v, 0, i)),
                pl.BlockSpec((bands, block), lambda v, i, p: (0, i)),
            ],
            out_specs=pl.BlockSpec((1, rows, block), lambda v, i, p: (v, 0, i)),
            scratch_shapes=[pltpu.VMEM((rows, block), jnp.float32)],
        ),
        out_shape=jax.ShapeDtypeStruct((count, rows, columns), out_dtype),
    )(present, mats, rhs, mask)


def split_bf16(values):
    high = lax.reduce_precision(values, exponent_bits=8, mantissa_bits=7)
    low = values - high
    return high.astype(jnp.bfloat16), low.astype(jnp.bfloat16)


def total_over(values, axes):
    count = lax.axis_size(axes)
    spread = jnp.broadcast_to(values[None, :], (count, values.shape[0]))
    return jnp.sum(lax.all_to_all(spread, axes, 0, 0, tiled=True), axis=0)


def filter_adjoint(pieces, lon_tiled, lat_tiled):
    half_lon = jnp.einsum(
        "vaxj,vablxt->vbljt", lon_tiled, pieces, preferred_element_type=jnp.float32
    ).astype(jnp.bfloat16)
    return jnp.einsum("vbljt,vbtk->vljk", half_lon, lat_tiled, preferred_element_type=jnp.float32)


def filter_forward(planes, lon_tiled, lat_tiled):
    smooth_lon = jnp.einsum(
        "vaxj,vljk->vlaxk", lon_tiled, planes, preferred_element_type=jnp.float32
    ).astype(jnp.bfloat16)
    return jnp.einsum(
        "vlaxm,vbtm->vablxt", smooth_lon, lat_tiled, preferred_element_type=jnp.float32
    ).astype(jnp.bfloat16)


def shards(innovations, obs_column, obs_scale, band_of_lat, balance, lon_filter, lat_filter):
    axes = ("gx", "gy")
    lon_parts = lax.axis_size("gx")
    lat_parts = lax.axis_size("gy")
    devices = lon_parts * lat_parts
    var_count, levels, obs_count = innovations.shape
    lon_full = lon_filter.shape[1]
    lat_full = lat_filter.shape[1]
    lon_tile = lon_full // lon_parts
    lat_tile = lat_full // lat_parts
    columns = lon_tile * lat_tile
    per_dev = levels // devices
    rows = var_count * levels
    lon_tiled = lon_filter.reshape(var_count, lon_parts, lon_tile, lon_full)
    lat_tiled = lat_filter.reshape(var_count, lat_parts, lat_tile, lat_full)
    inv_scale = obs_scale[:, :, None]
    one_hot = (
        obs_column[:, None] == jnp.arange(columns, dtype=jnp.int32)[None, :]
    ).astype(jnp.bfloat16)
    bands = balance.shape[0]
    band_hot = (
        band_of_lat[None, :] == jnp.arange(bands, dtype=jnp.int32)[:, None]
    ).astype(jnp.bfloat16)
    band_present = jnp.max(band_hot, axis=1).astype(jnp.int32)
    band_mask = jnp.broadcast_to(band_hot[:, None, :], (bands, lon_tile, lat_tile)).reshape(bands, columns)
    balance_adj = jnp.transpose(balance, (1, 0, 3, 2))
    balance_fwd = jnp.transpose(balance, (1, 0, 2, 3))
    control = None
    increment = None
    inc_obs = None
    for iteration in range(ITERS):
        if inc_obs is None:
            scaled = -innovations * inv_scale
        else:
            scaled = (inc_obs - innovations) * inv_scale
        weighted = jnp.clip(scaled, -huber_edge, huber_edge) * inv_scale
        forcing = jnp.dot(
            weighted.reshape(rows, obs_count).astype(jnp.bfloat16),
            one_hot,
            preferred_element_type=jnp.float32,
        ).astype(jnp.bfloat16)
        forcing = forcing.reshape(var_count, levels, columns)
        grad_parts = []
        gradients = []
        returns = []
        obs_parts = []
        balanced_all = band_mix(band_present, balance_adj, forcing, band_mask, jnp.bfloat16, block=columns)
        for var in range(var_count):
            balanced = balanced_all[var]
            pieces = lax.all_to_all(
                balanced.reshape(devices, 2, per_dev * columns // 2), axes, 0, 0, tiled=True
            )
            tiled = pieces.reshape(lon_parts, lat_parts, per_dev, lon_tile, lat_tile)
            half_lon = jnp.einsum(
                "axj,ablxt->bljt", lon_tiled[var], tiled, preferred_element_type=jnp.float32
            ).astype(jnp.bfloat16)
            adjoint = jnp.einsum("bljt,btk->ljk", half_lon, lat_tiled[var], preferred_element_type=jnp.float32)
            gradient = adjoint if control is None else control[var] + adjoint
            grad_parts.append(jnp.sum(gradient * gradient))
            gradients.append(gradient)
            smooth_lon = jnp.einsum(
                "axj,ljk->laxk", lon_tiled[var], gradient.astype(jnp.bfloat16), preferred_element_type=jnp.float32
            ).astype(jnp.bfloat16)
            smoothed = jnp.einsum(
                "laxm,btm->ablxt", smooth_lon, lat_tiled[var], preferred_element_type=jnp.float32
            ).astype(jnp.bfloat16)
            returned = lax.all_to_all(
                smoothed.reshape(devices, 2, per_dev * columns // 2), axes, 0, 0, tiled=True
            ).reshape(levels, columns)
            response_var = band_mix(
                band_present, balance_fwd[var : var + 1], returned[None], band_mask, jnp.float32, block=columns
            )[0]
            returns.append(response_var)
            r_high, r_low = split_bf16(response_var)
            obs_parts.append(
                jnp.einsum("lc,jc->lj", r_high, one_hot, preferred_element_type=jnp.float32)
                + jnp.einsum("lc,jc->lj", r_low, one_hot, preferred_element_type=jnp.float32)
            )
        response = jnp.stack(returns)
        at_obs = jnp.stack(obs_parts)
        gradient = jnp.stack(gradients)
        grad_local = sum(grad_parts)
        weight = huber_edge / jnp.maximum(jnp.abs(scaled), huber_edge)
        curve_local = jnp.sum(weight * (inv_scale * at_obs) ** 2)
        totals = total_over(jnp.stack([grad_local, curve_local]), axes)
        grad_norm = totals[0]
        curvature = totals[1]
        step_size = grad_norm / (grad_norm + curvature)
        if control is None:
            control = -(step_size * gradient)
            increment = -(step_size * response)
            inc_obs = -(step_size * at_obs)
        else:
            control = control - step_size * gradient
            increment = increment - step_size * response
            inc_obs = inc_obs - step_size * at_obs
    return (control, increment.reshape(var_count, levels, lon_tile, lat_tile))


def solution(mesh):
    in_specs = (P(None, None, ("gx", "gy")), P(("gx", "gy")), P(), P("gy"), P(), P(), P())
    out_specs = (P(None, ("gx", "gy"), None, None), P(None, None, "gx", "gy"))
    return jax.shard_map(shards, mesh=mesh, in_specs=in_specs, out_specs=out_specs, check_vma=False)
```

```python
import jax
import jax.numpy as jnp
from jax import lax
from jax.sharding import PartitionSpec as P
from jax.experimental import pallas as pl
from jax.experimental.pallas import tpu as pltpu

ITERS = 2


huber_edge = 1.5


def _band_mix_kernel(present_ref, mat_ref, rhs_ref, mask_ref, out_ref, acc_ref):
    acc_ref[...] = jnp.zeros(acc_ref.shape, jnp.float32)
    for band in range(mat_ref.shape[1]):

        @pl.when(present_ref[band] > 0)
        def _():
            masked = rhs_ref[0] * mask_ref[band : band + 1, :]
            acc_ref[...] += jnp.dot(mat_ref[0, band], masked, preferred_element_type=jnp.float32)

    out_ref[0] = acc_ref[...].astype(out_ref.dtype)


def band_mix(present, mats, rhs, mask, out_dtype, block=2048):
    count, bands, rows, inner = mats.shape
    columns = rhs.shape[2]
    return pl.pallas_call(
        _band_mix_kernel,
        grid_spec=pltpu.PrefetchScalarGridSpec(
            num_scalar_prefetch=1,
            grid=(count, columns // block),
            in_specs=[
                pl.BlockSpec((1, bands, rows, inner), lambda v, i, p: (v, 0, 0, 0)),
                pl.BlockSpec((1, inner, block), lambda v, i, p: (v, 0, i)),
                pl.BlockSpec((bands, block), lambda v, i, p: (0, i)),
            ],
            out_specs=pl.BlockSpec((1, rows, block), lambda v, i, p: (v, 0, i)),
            scratch_shapes=[pltpu.VMEM((rows, block), jnp.float32)],
        ),
        out_shape=jax.ShapeDtypeStruct((count, rows, columns), out_dtype),
    )(present, mats, rhs, mask)


def split_bf16(values):
    high = lax.reduce_precision(values, exponent_bits=8, mantissa_bits=7)
    low = values - high
    return high.astype(jnp.bfloat16), low.astype(jnp.bfloat16)


def total_over(values, axes):
    count = lax.axis_size(axes)
    spread = jnp.broadcast_to(values[None, :], (count, values.shape[0]))
    return jnp.sum(lax.all_to_all(spread, axes, 0, 0, tiled=True), axis=0)


def filter_adjoint(pieces, lon_tiled, lat_tiled):
    half_lon = jnp.einsum(
        "vaxj,vablxt->vbljt", lon_tiled, pieces, preferred_element_type=jnp.float32
    ).astype(jnp.bfloat16)
    return jnp.einsum("vbljt,vbtk->vljk", half_lon, lat_tiled, preferred_element_type=jnp.float32)


def filter_forward(planes, lon_tiled, lat_tiled):
    smooth_lon = jnp.einsum(
        "vaxj,vljk->vlaxk", lon_tiled, planes, preferred_element_type=jnp.float32
    ).astype(jnp.bfloat16)
    return jnp.einsum(
        "vlaxm,vbtm->vablxt", smooth_lon, lat_tiled, preferred_element_type=jnp.float32
    ).astype(jnp.bfloat16)


def shards(innovations, obs_column, obs_scale, band_of_lat, balance, lon_filter, lat_filter):
    axes = ("gx", "gy")
    lon_parts = lax.axis_size("gx")
    lat_parts = lax.axis_size("gy")
    devices = lon_parts * lat_parts
    var_count, levels, obs_count = innovations.shape
    lon_full = lon_filter.shape[1]
    lat_full = lat_filter.shape[1]
    lon_tile = lon_full // lon_parts
    lat_tile = lat_full // lat_parts
    columns = lon_tile * lat_tile
    per_dev = levels // devices
    rows = var_count * levels
    lon_tiled = lon_filter.reshape(var_count, lon_parts, lon_tile, lon_full)
    lat_tiled = lat_filter.reshape(var_count, lat_parts, lat_tile, lat_full)
    inv_scale = obs_scale[:, :, None]
    one_hot = (
        obs_column[:, None] == jnp.arange(columns, dtype=jnp.int32)[None, :]
    ).astype(jnp.bfloat16)
    bands = balance.shape[0]
    band_hot = (
        band_of_lat[None, :] == jnp.arange(bands, dtype=jnp.int32)[:, None]
    ).astype(jnp.bfloat16)
    band_present = jnp.max(band_hot, axis=1).astype(jnp.int32)
    band_mask = jnp.broadcast_to(band_hot[:, None, :], (bands, lon_tile, lat_tile)).reshape(bands, columns)
    balance_adj = jnp.transpose(balance, (1, 0, 3, 2))
    balance_fwd = jnp.transpose(balance, (1, 0, 2, 3))
    one_hot_pair = jnp.concatenate([one_hot, one_hot], axis=0)
    control = None
    increment = None
    inc_obs = None
    for iteration in range(ITERS):
        if inc_obs is None:
            scaled = -innovations * inv_scale
        else:
            scaled = (inc_obs - innovations) * inv_scale
        weighted = jnp.clip(scaled, -huber_edge, huber_edge) * inv_scale
        w_high, w_low = split_bf16(weighted.reshape(rows, obs_count))
        forcing = jnp.dot(
            jnp.concatenate([w_high, w_low], axis=1),
            one_hot_pair,
            preferred_element_type=jnp.float32,
        ).astype(jnp.bfloat16)
        forcing = forcing.reshape(var_count, levels, columns)
        grad_parts = []
        gradients = []
        returns = []
        obs_parts = []
        balanced_all = band_mix(band_present, balance_adj, forcing, band_mask, jnp.bfloat16, block=columns)
        for var in range(var_count):
            balanced = balanced_all[var]
            pieces = lax.all_to_all(
                balanced.reshape(devices, 2, per_dev * columns // 2), axes, 0, 0, tiled=True
            )
            tiled = pieces.reshape(lon_parts, lat_parts, per_dev, lon_tile, lat_tile)
            half_lon = jnp.einsum(
                "axj,ablxt->bljt", lon_tiled[var], tiled, preferred_element_type=jnp.float32
            ).astype(jnp.bfloat16)
            adjoint = jnp.einsum("bljt,btk->ljk", half_lon, lat_tiled[var], preferred_element_type=jnp.float32)
            gradient = adjoint if control is None else control[var] + adjoint
            grad_parts.append(jnp.sum(gradient * gradient))
            gradients.append(gradient)
            smooth_lon = jnp.einsum(
                "axj,ljk->laxk", lon_tiled[var], gradient.astype(jnp.bfloat16), preferred_element_type=jnp.float32
            ).astype(jnp.bfloat16)
            smoothed = jnp.einsum(
                "laxm,btm->ablxt", smooth_lon, lat_tiled[var], preferred_element_type=jnp.float32
            ).astype(jnp.bfloat16)
            returned = lax.all_to_all(
                smoothed.reshape(devices, 2, per_dev * columns // 2), axes, 0, 0, tiled=True
            ).reshape(levels, columns)
            response_var = band_mix(
                band_present, balance_fwd[var : var + 1], returned[None], band_mask, jnp.float32, block=columns
            )[0]
            returns.append(response_var)
            if iteration == ITERS - 1:
                obs_parts.append(
                    jnp.einsum(
                        "lc,jc->lj", response_var.astype(jnp.bfloat16), one_hot, preferred_element_type=jnp.float32
                    )
                )
            else:
                r_high, r_low = split_bf16(response_var)
                obs_parts.append(
                    jnp.einsum("lc,jc->lj", r_high, one_hot, preferred_element_type=jnp.float32)
                    + jnp.einsum("lc,jc->lj", r_low, one_hot, preferred_element_type=jnp.float32)
                )
        response = jnp.stack(returns)
        at_obs = jnp.stack(obs_parts)
        gradient = jnp.stack(gradients)
        grad_local = sum(grad_parts)
        weight = huber_edge / jnp.maximum(jnp.abs(scaled), huber_edge)
        curve_local = jnp.sum(weight * (inv_scale * at_obs) ** 2)
        totals = total_over(jnp.stack([grad_local, curve_local]), axes)
        grad_norm = totals[0]
        curvature = totals[1]
        step_size = grad_norm / (grad_norm + curvature)
        if control is None:
            control = -(step_size * gradient)
            increment = -(step_size * response)
            inc_obs = -(step_size * at_obs)
        else:
            control = control - step_size * gradient
            increment = increment - step_size * response
            inc_obs = inc_obs - step_size * at_obs
    return (control, increment.reshape(var_count, levels, lon_tile, lat_tile))


def solution(mesh):
    in_specs = (P(None, None, ("gx", "gy")), P(("gx", "gy")), P(), P("gy"), P(), P(), P())
    out_specs = (P(None, ("gx", "gy"), None, None), P(None, None, "gx", "gy"))
    return jax.shard_map(shards, mesh=mesh, in_specs=in_specs, out_specs=out_specs, check_vma=False)
```
